512 devices in a mesh: ctx: 64 (over z_lo, y, core), ch: 8 (over z_hi, x).
Axes of the slice: x: 4, y: 8, z: 8 (z_hi: 2, z_lo: 4; z = z_hi * 4 + z_lo), core: 2. Of those that a mesh axis runs over, the one named last changes fastest.
Arguments:
- query_in: bfloat16 [16384, 4096], P('ctx', 'ch'), may hold values from -6 to 6
- key_in: bfloat16 [16384, 4096], P('ctx', 'ch'), may hold values from -6 to 6
- value_in: bfloat16 [16384, 4096], P('ctx', 'ch'), may hold values from -6 to 6
- short_weight: float32 [3, 3, 4096], P(None, None, 'ch'), may hold values from -3 to 3
- long_filter: bfloat16 [32, 768], P('ch'), may hold values from -1.1 to 1.1
- skip_weight: float32 [4096], P('ch'), may hold values from -1 to 1
- out_weight: bfloat16 [4096, 4096], P('ctx', 'ch'), may hold values from -0.09375 to 0.09375
- doc_ids: int32 [16384], P('ctx'), may hold values from 0 to 41, as said below
- out_grad: bfloat16 [16384, 4096], P('ctx', 'ch'), may hold values from -6 to 6
Outputs:
- layer_out: bfloat16 [16384, 4096], P('ctx', 'ch')
- grad_query: bfloat16 [16384, 4096], P('ctx', 'ch')
- grad_key: bfloat16 [16384, 4096], P('ctx', 'ch')
- grad_value: bfloat16 [16384, 4096], P('ctx', 'ch')
The draws below stay inside these ranges and needn't reach their ends.
Inputs may be any that keep to these rules, and one draw needn't show every extreme that they name: doc_ids never falls along the tokens; every number from 0 to 41 occurs; every document has at most 768 tokens and one has exactly 768.
All inputs are finite; a program needn't handle non-finite values.
Results may differ from the reference program's by a relative error of at most 0.0058.
Values may be sent and summed in bfloat16 or wider, within the bound.
No kernel may reach another device: no remote copies, remote signals or barrier semaphores. Data moves between devices by JAX's collectives and lax.ppermute only.
A program may use at most 64 MiB of HBM per device.

```python
import jax
import jax.numpy as jnp
from jax import lax

D = 4096
FGROUP = 128
ROWS = 256
HOPS = 3
TAP_SPAN = 768
TOKENS = 16384
FILTER_GROUPS = 32
DOCS = 42


def draw_long_filter(key, part):
    random_subkeys = jax.random.split(key, 6)
    lag_positions = jnp.arange(TAP_SPAN, dtype=jnp.float32)[None, :]
    fast_share = 0.5
    is_fast = jax.random.uniform(random_subkeys[0], (FILTER_GROUPS, 1)) < fast_share
    fast_decay = jax.random.uniform(random_subkeys[1], (FILTER_GROUPS, 1), minval=30.0, maxval=50.0)
    slow_decay = jnp.exp(jax.random.uniform(random_subkeys[2], (FILTER_GROUPS, 1), minval=jnp.log(1.0 * TAP_SPAN), maxval=jnp.log(10.0 * TAP_SPAN)))
    decay_len = jnp.where(is_fast, fast_decay, slow_decay)
    decay_envelope = jnp.exp(-lag_positions / decay_len)
    spike_position = jax.random.uniform(random_subkeys[3], (FILTER_GROUPS, 3)) * TAP_SPAN
    spike_mask = jax.random.uniform(random_subkeys[4], (FILTER_GROUPS, 3), minval=0.5, maxval=0.8)
    for spike_index in range(3):
        decay_envelope = decay_envelope * jnp.where(lag_positions > spike_position[:, spike_index:spike_index + 1], spike_mask[:, spike_index:spike_index + 1], 1.0)
    norm_scale = jnp.sqrt((1.0 - jnp.exp(-2.0 / decay_len)) / (1.0 - jnp.exp(-2.0 * TAP_SPAN / decay_len)))
    rough_part = jnp.clip(jax.random.normal(random_subkeys[5], (FILTER_GROUPS, TAP_SPAN)), -4.0, 4.0)
    return (rough_part * decay_envelope * norm_scale).astype(jnp.bfloat16)


def draw_doc_ids(key, part):
    first_key = jax.random.fold_in(key, 11)
    jitter_key = jax.random.fold_in(key, 12)
    block_total = TOKENS // ROWS
    first_len = jax.random.randint(first_key, (), 1, ROWS // 4 + 1).astype(jnp.int32)
    region_start = first_len + TAP_SPAN
    middle_cut = jnp.int32(block_total // 2 * ROWS + ROWS // 2)
    remaining = DOCS - 2
    region_len = TOKENS - region_start
    lower_docs = (2 * remaining * (middle_cut - region_start) + region_len) // (2 * region_len)
    lower_docs = jnp.clip(lower_docs, 1, remaining - 1).astype(jnp.int32)
    upper_docs = (remaining - lower_docs).astype(jnp.int32)
    cut_index = jnp.arange(DOCS - 3, dtype=jnp.int32)
    lower_step = (middle_cut - region_start) // lower_docs
    upper_step = (TOKENS - middle_cut) // upper_docs
    lower_cuts = region_start + (cut_index + 1) * (middle_cut - region_start) // lower_docs
    upper_index = cut_index - lower_docs + 1
    upper_cuts = middle_cut + upper_index * (TOKENS - middle_cut) // upper_docs
    in_lower = cut_index < lower_docs - 1
    half_width = jnp.where(in_lower, lower_step // 8, upper_step // 8)
    raw_bits = jax.random.randint(jitter_key, (DOCS - 3,), 0, 1 << 20).astype(jnp.int32)
    jitter = raw_bits % (2 * half_width + 1) - half_width
    cuts = jnp.where(in_lower, lower_cuts + jitter, jnp.where(cut_index == lower_docs - 1, middle_cut, upper_cuts + jitter))
    bounds = jnp.concatenate([jnp.stack([first_len, region_start]), cuts.astype(jnp.int32)])
    positions = jnp.arange(TOKENS, dtype=jnp.int32)
    return jnp.sum((positions[:, None] >= bounds[None, :]).astype(jnp.int32), axis=1).astype(jnp.int32)


def block_scale(stream_key, extent, cuts, least, top_value):
    loudness, own = 1.0, jax.random.fold_in(stream_key, 6)
    for axis_at, parts in cuts:
        draws = jnp.exp(jax.random.uniform(jax.random.fold_in(own, axis_at), (parts,), jnp.float32, least / len(cuts), top_value / len(cuts)))
        loudness = loudness * jnp.repeat(draws, extent[axis_at] // parts).reshape([-1 if axis == axis_at else 1 for axis in range(len(extent))])
    return loudness


def normal_values(own_key, shape, scale, reach, cuts=(), held_as=jnp.bfloat16):
    drawn = jax.random.normal(own_key, shape, jnp.float32) * scale
    if len(cuts) > 0:
        drawn = block_scale(own_key, shape, cuts, -0.22, 0.18) * drawn
    return jnp.clip(drawn, min=-reach, max=reach).astype(held_as)


def setup_inputs(seed: int = 0) -> dict:
    key_list = jax.random.split(jax.random.key(seed), 10)
    return {
        "query_in": normal_values(key_list[0], (TOKENS, D), 1.0, 6.0, ((0, 64), (1, 8))),
        "key_in": normal_values(key_list[1], (TOKENS, D), 1.0, 6.0, ((0, 64), (1, 8))),
        "value_in": normal_values(key_list[2], (TOKENS, D), 1.0, 6.0, ((0, 64), (1, 8))),
        "short_weight": normal_values(key_list[3], (3, 3, D), 0.6, 3.0, ((2, 8),), jnp.float32),
        "long_filter": draw_long_filter(jax.random.fold_in(key_list[9], 71), 0),
        "skip_weight": jnp.clip(jax.random.uniform(key_list[5], (D,), jnp.float32, -1.0, 1.0) * block_scale(key_list[5], (D,), ((0, 8),), -0.4, 0.0), -1.0, 1.0),
        "out_weight": normal_values(key_list[6], (D, D), D ** -0.5, 0.09375, ((0, 64), (1, 8))),
        "doc_ids": draw_doc_ids(jax.random.fold_in(key_list[9], 71), 0),
        "out_grad": normal_values(key_list[8], (TOKENS, D), 1.0, 6.0, ((0, 64), (1, 8))),
    }


def causal_taps(values, weights, doc_ids):
    total_rows = values.shape[0]
    widened = values.astype(jnp.float32)
    summed = jnp.zeros(widened.shape, jnp.float32)
    for offset in range(3):
        shifted = jnp.concatenate([jnp.zeros((offset, widened.shape[1]), jnp.float32), widened[:total_rows - offset]], axis=0)
        shifted_ids = jnp.concatenate([jnp.full((offset,), -1, jnp.int32), doc_ids[:total_rows - offset].astype(jnp.int32)])
        same_doc = shifted_ids == doc_ids.astype(jnp.int32)
        summed = summed + jnp.where(same_doc[:, None], weights[offset][None, :] * shifted, 0.0)
    return summed


def anti_taps(values, weights, doc_ids):
    total_rows = values.shape[0]
    widened = values.astype(jnp.float32)
    summed = jnp.zeros(widened.shape, jnp.float32)
    for offset in range(3):
        shifted = jnp.concatenate([widened[offset:], jnp.zeros((offset, widened.shape[1]), jnp.float32)], axis=0)
        shifted_ids = jnp.concatenate([doc_ids[offset:].astype(jnp.int32), jnp.full((offset,), -1, jnp.int32)])
        same_doc = shifted_ids == doc_ids.astype(jnp.int32)
        summed = summed + jnp.where(same_doc[:, None], weights[offset][None, :] * shifted, 0.0)
    return summed


def band_conv(values, long_filter, doc_ids, adjoint):
    total_rows, channels = values.shape
    blocks = total_rows // ROWS
    block_ids = doc_ids.astype(jnp.int32).reshape(blocks, ROWS)
    row_index = jnp.arange(ROWS, dtype=jnp.int32)

    def one_group(group_index):
        columns = lax.dynamic_slice_in_dim(values, group_index * FGROUP, FGROUP, 1).astype(jnp.float32).reshape(blocks, ROWS, FGROUP)
        filter_taps = lax.dynamic_index_in_dim(long_filter, group_index, 0, keepdims=False).astype(jnp.float32)
        summed = jnp.zeros((blocks, ROWS, FGROUP), jnp.float32)
        for distance in range(HOPS + 1):
            lag_table = distance * ROWS + row_index[:, None] - row_index[None, :]
            band_tile = jnp.where((lag_table >= 0) & (lag_table < TAP_SPAN), filter_taps[jnp.clip(lag_table, 0, TAP_SPAN - 1)], 0.0)
            source_ids = jnp.concatenate([jnp.full((distance, ROWS), -1, jnp.int32), block_ids[:blocks - distance]], axis=0)
            weights = jnp.where(block_ids[:, :, None] == source_ids[:, None, :], band_tile[None], 0.0)
            if adjoint:
                carried = jnp.einsum("bts,btc->bsc", weights, columns)
                summed = summed + jnp.concatenate([carried[distance:], jnp.zeros((distance, ROWS, FGROUP), jnp.float32)], axis=0)
            else:
                source = jnp.concatenate([jnp.zeros((distance, ROWS, FGROUP), jnp.float32), columns[:blocks - distance]], axis=0)
                summed = summed + jnp.einsum("bts,bsc->btc", weights, source)
        return summed.reshape(total_rows, FGROUP)

    stacked = lax.map(one_group, jnp.arange(FILTER_GROUPS, dtype=jnp.int32))
    return jnp.transpose(stacked, (1, 0, 2)).reshape(total_rows, channels)


def reference(query_in, key_in, value_in, short_weight, long_filter, skip_weight, out_weight, doc_ids, out_grad):
    query_short = causal_taps(query_in, short_weight[0], doc_ids)
    key_short = causal_taps(key_in, short_weight[1], doc_ids)
    value_short = causal_taps(value_in, short_weight[2], doc_ids)
    gated = (key_short * value_short).astype(jnp.bfloat16)
    mixed = band_conv(gated, long_filter, doc_ids, False) + skip_weight[None, :] * gated.astype(jnp.float32)
    pre_gate = (query_short * mixed).astype(jnp.bfloat16)
    layer_out = jnp.dot(pre_gate, out_weight, preferred_element_type=jnp.float32).astype(jnp.bfloat16)
    grad_pre = jnp.dot(out_grad, out_weight.T, preferred_element_type=jnp.float32)
    grad_query_short = (grad_pre * mixed).astype(jnp.bfloat16)
    grad_mixed = (grad_pre * query_short).astype(jnp.bfloat16)
    grad_gated = band_conv(grad_mixed, long_filter, doc_ids, True) + skip_weight[None, :] * grad_mixed.astype(jnp.float32)
    grad_key_short = (grad_gated * value_short).astype(jnp.bfloat16)
    grad_value_short = (grad_gated * key_short).astype(jnp.bfloat16)
    grad_query = anti_taps(grad_query_short, short_weight[0], doc_ids).astype(jnp.bfloat16)
    grad_key = anti_taps(grad_key_short, short_weight[1], doc_ids).astype(jnp.bfloat16)
    grad_value = anti_taps(grad_value_short, short_weight[2], doc_ids).astype(jnp.bfloat16)
    return (layer_out, grad_query, grad_key, grad_value)
```

```python
import jax
import jax.numpy as jnp
from jax import lax
from jax.sharding import Mesh, PartitionSpec as P

HOPS = 3
CHIPS = ("zl", "y")
CTX = ("zl", "y", "core")
CH = ("zh", "x")


def gather_weight(out_weight, chip_count):
    spread = jnp.broadcast_to(out_weight[None], (chip_count,) + out_weight.shape)
    mine = lax.all_to_all(spread, CHIPS, 0, 0, tiled=True).reshape(-1, out_weight.shape[1])
    other = lax.ppermute(mine, "core", [(0, 1), (1, 0)])
    return mine, other, lax.axis_index("core")


def shifted(array, axis, by):
    size = lax.axis_size(axis)
    pairs = [(i, i + by) for i in range(size) if 0 <= i + by < size]
    return lax.ppermute(array, axis, pairs)


def toeplitz_tiles(long_filter, row_count, hop_count):
    group_count, span_len = long_filter.shape
    padded = jnp.concatenate(
        [
            jnp.zeros((group_count, row_count), long_filter.dtype),
            long_filter,
            jnp.zeros((group_count, (hop_count + 3) * row_count - span_len), long_filter.dtype),
        ],
        axis=1,
    )
    tiles_list = []
    for distance in range(hop_count + 1):
        window = padded[:, distance * row_count + 1 : distance * row_count + 1 + 2 * row_count]
        cyclic = jnp.concatenate(
            [
                window[:, row_count - 1 : 2 * row_count - 1],
                jnp.zeros((group_count, 1), window.dtype),
                window[:, : row_count - 1],
            ],
            axis=1,
        )
        repeated = jnp.tile(cyclic, (1, row_count))[:, : row_count * (2 * row_count - 1)]
        tiles_list.append(
            repeated.reshape(group_count, row_count, 2 * row_count - 1)[:, :, :row_count]
        )
    return tiles_list


def apply_forward(band_tile, source):
    row_count, channels = source.shape
    grouped = source.reshape(row_count, band_tile.shape[0], -1)
    return jnp.einsum(
        "gst,sgc->tgc", band_tile, grouped, preferred_element_type=jnp.float32
    ).reshape(row_count, channels)


def apply_adjoint(band_tile, source):
    row_count, channels = source.shape
    grouped = source.reshape(row_count, band_tile.shape[0], -1)
    return jnp.einsum(
        "gst,tgc->sgc", band_tile, grouped, preferred_element_type=jnp.float32
    ).reshape(row_count, channels)


def causal_taps(extended, weights, ext_ids, doc_ids):
    row_count = doc_ids.shape[0]
    summed = jnp.zeros((row_count, extended.shape[1]), jnp.float32)
    for offset in range(3):
        first_row = 2 - offset
        same_doc = ext_ids[first_row : first_row + row_count] == doc_ids
        summed = summed + jnp.where(
            same_doc[:, None],
            weights[offset][None, :]
            * extended[first_row : first_row + row_count].astype(jnp.float32),
            0.0,
        )
    return summed


def anti_taps(extended, weights, ext_ids, doc_ids):
    row_count = doc_ids.shape[0]
    summed = jnp.zeros((row_count, extended.shape[1]), jnp.float32)
    for offset in range(3):
        same_doc = ext_ids[offset : offset + row_count] == doc_ids
        summed = summed + jnp.where(
            same_doc[:, None],
            weights[offset][None, :] * extended[offset : offset + row_count].astype(jnp.float32),
            0.0,
        )
    return summed


def local(
    query_in,
    key_in,
    value_in,
    short_weight,
    long_filter,
    skip_weight,
    out_weight,
    doc_ids,
    out_grad,
):
    row_count, channels = query_in.shape
    before_ids = shifted(doc_ids[-2:] + 1, CTX, 1) - 1
    after_ids = shifted(doc_ids[:2] + 1, CTX, -1) - 1
    first_id = doc_ids[0]
    last_id = doc_ids[-1]
    prev_last = before_ids[1]
    next_first = after_ids[0]
    single_doc = first_id == last_id
    joins_next = next_first == last_id
    joins_prev = prev_last == first_id
    prev_rows = shifted((query_in[-2:], key_in[-2:], value_in[-2:]), CTX, 1)
    back_ids = jnp.concatenate([before_ids, doc_ids])
    query_short = causal_taps(
        jnp.concatenate([prev_rows[0], query_in]), short_weight[0], back_ids, doc_ids
    )
    key_short = causal_taps(
        jnp.concatenate([prev_rows[1], key_in]), short_weight[1], back_ids, doc_ids
    )
    value_short = causal_taps(
        jnp.concatenate([prev_rows[2], value_in]), short_weight[2], back_ids, doc_ids
    )
    gated = (key_short * value_short).astype(jnp.bfloat16)
    tiles_list = toeplitz_tiles(long_filter, row_count, HOPS)
    same_doc = doc_ids[:, None] == doc_ids[None, :]
    diagonal = jnp.where(same_doc[None], tiles_list[0], jnp.zeros((), tiles_list[0].dtype))
    head_rows = (doc_ids == first_id)[:, None]
    tail_rows = (doc_ids == last_id)[:, None]
    zero_half = jnp.zeros((), gated.dtype)

    def cross_term(is_live, product, band_tile, source):
        summand = jnp.where(is_live, product(band_tile, source), 0.0)
        return summand

    mixed = apply_forward(diagonal, gated) + skip_weight[None, :] * gated.astype(jnp.float32)
    own_tail = jnp.where(tail_rows, gated, zero_half)
    moving = jnp.where(joins_next, own_tail, zero_half)
    for distance in range(1, HOPS + 1):
        moving = shifted(moving, CTX, 1)
        is_live = jnp.any(moving != 0)
        mixed = mixed + jnp.where(
            head_rows, cross_term(is_live, apply_forward, tiles_list[distance], moving), 0.0
        )
        moving = jnp.where(single_doc & joins_next, moving, zero_half)
    pre_gate = (query_short * mixed).astype(jnp.bfloat16)
    pair_size = lax.axis_size("core")
    chip_count = lax.axis_size(CHIPS)
    weight_rows, weight_rows_other, core_index = gather_weight(out_weight, chip_count)
    ch_count = lax.axis_size(CH)
    spread = jnp.broadcast_to(pre_gate[None], (ch_count,) + pre_gate.shape)
    gathered = lax.all_to_all(spread, CH, 0, 0, tiled=True).reshape(
        ch_count, row_count, channels
    )
    full_pre = jnp.transpose(gathered, (1, 0, 2)).reshape(
        row_count, chip_count, pair_size, out_weight.shape[0]
    )
    pre_first = full_pre[:, :, 0].reshape(row_count, -1)
    pre_second = full_pre[:, :, 1].reshape(row_count, -1)
    on_first = core_index == 0
    pre_mine = jnp.where(on_first, pre_first, pre_second)
    pre_other = jnp.where(on_first, pre_second, pre_first)
    out_sum = jnp.dot(pre_mine, weight_rows, preferred_element_type=jnp.float32) + jnp.dot(
        pre_other, weight_rows_other, preferred_element_type=jnp.float32
    )
    dims = (((1,), (1,)), ((), ()))
    part_mine = lax.dot_general(
        weight_rows, out_grad, dims, preferred_element_type=jnp.float32
    ).reshape(chip_count, 1, -1, row_count)
    part_other = lax.dot_general(
        weight_rows_other, out_grad, dims, preferred_element_type=jnp.float32
    ).reshape(chip_count, 1, -1, row_count)
    partial = jnp.where(
        on_first,
        jnp.concatenate([part_mine, part_other], axis=1),
        jnp.concatenate([part_other, part_mine], axis=1),
    ).reshape(-1, row_count)
    grad_cols = lax.psum_scatter(partial, CH, scatter_dimension=0, tiled=True)
    layer_out = out_sum.astype(jnp.bfloat16)
    grad_pre = jnp.transpose(grad_cols)
    grad_query_short = (grad_pre * mixed).astype(jnp.bfloat16)
    grad_mixed = (grad_pre * query_short).astype(jnp.bfloat16)
    own_head = jnp.where(head_rows, grad_mixed, zero_half)
    grad_gated = apply_adjoint(diagonal, grad_mixed) + skip_weight[None, :] * grad_mixed.astype(
        jnp.float32
    )
    moving_back = jnp.where(joins_prev, own_head, zero_half)
    for distance in range(1, HOPS + 1):
        moving_back = shifted(moving_back, CTX, -1)
        is_live = jnp.any(moving_back != 0)
        grad_gated = grad_gated + jnp.where(
            tail_rows, cross_term(is_live, apply_adjoint, tiles_list[distance], moving_back), 0.0
        )
        moving_back = jnp.where(single_doc & joins_prev, moving_back, zero_half)
    grad_key_short = (grad_gated * value_short).astype(jnp.bfloat16)
    grad_value_short = (grad_gated * key_short).astype(jnp.bfloat16)
    next_rows = shifted((grad_query_short[:2], grad_key_short[:2], grad_value_short[:2]), CTX, -1)
    ahead_ids = jnp.concatenate([doc_ids, after_ids])
    grad_query = anti_taps(
        jnp.concatenate([grad_query_short, next_rows[0]]), short_weight[0], ahead_ids, doc_ids
    ).astype(jnp.bfloat16)
    grad_key = anti_taps(
        jnp.concatenate([grad_key_short, next_rows[1]]), short_weight[1], ahead_ids, doc_ids
    ).astype(jnp.bfloat16)
    grad_value = anti_taps(
        jnp.concatenate([grad_value_short, next_rows[2]]), short_weight[2], ahead_ids, doc_ids
    ).astype(jnp.bfloat16)
    return (layer_out, grad_query, grad_key, grad_value)


def solution(mesh):
    zl, y, core = 4, 8, 2
    split_mesh = Mesh(
        mesh.devices.reshape(zl, y, core, mesh.devices.shape[1] // 4, 4),
        ("zl", "y", "core", "zh", "x"),
    )
    return jax.shard_map(
        local,
        mesh=split_mesh,
        in_specs=(
            P(CTX, CH),
            P(CTX, CH),
            P(CTX, CH),
            P(None, None, CH),
            P(CH, None),
            P(CH),
            P(CTX, CH),
            P(CTX),
            P(CTX, CH),
        ),
        out_specs=(P(CTX, CH), P(CTX, CH), P(CTX, CH), P(CTX, CH)),
        check_vma=False,
    )
```

```python
import jax
import jax.numpy as jnp
from jax import lax
from jax.sharding import Mesh, PartitionSpec as P

HOPS = 3
CHIPS = ("zl", "y")
CTX = ("zl", "y", "core")
CH = ("zh", "x")


def gather_weight(out_weight, chip_count):
    spread = jnp.broadcast_to(out_weight[None], (chip_count,) + out_weight.shape)
    mine = lax.all_to_all(spread, CHIPS, 0, 0, tiled=True).reshape(-1, out_weight.shape[1])
    other = lax.ppermute(mine, "core", [(0, 1), (1, 0)])
    return mine, other, lax.axis_index("core")


def shifted(array, axis, by):
    size = lax.axis_size(axis)
    pairs = [(i, i + by) for i in range(size) if 0 <= i + by < size]
    return lax.ppermute(array, axis, pairs)


def toeplitz_tiles(long_filter, row_count, hop_count):
    group_count, span_len = long_filter.shape
    padded = jnp.concatenate(
        [
            jnp.zeros((group_count, row_count), long_filter.dtype),
            long_filter,
            jnp.zeros((group_count, (hop_count + 3) * row_count - span_len), long_filter.dtype),
        ],
        axis=1,
    )
    tiles_list = []
    for distance in range(hop_count + 1):
        window = padded[:, distance * row_count + 1 : distance * row_count + 1 + 2 * row_count]
        cyclic = jnp.concatenate(
            [
                window[:, row_count - 1 : 2 * row_count - 1],
                jnp.zeros((group_count, 1), window.dtype),
                window[:, : row_count - 1],
            ],
            axis=1,
        )
        repeated = jnp.tile(cyclic, (1, row_count))[:, : row_count * (2 * row_count - 1)]
        tiles_list.append(
            repeated.reshape(group_count, row_count, 2 * row_count - 1)[:, :, :row_count]
        )
    return tiles_list


def apply_forward(band_tile, source):
    row_count, channels = source.shape
    grouped = source.reshape(row_count, band_tile.shape[0], -1)
    return jnp.einsum(
        "gst,sgc->tgc", band_tile, grouped, preferred_element_type=jnp.float32
    ).reshape(row_count, channels)


def apply_adjoint(band_tile, source):
    row_count, channels = source.shape
    grouped = source.reshape(row_count, band_tile.shape[0], -1)
    return jnp.einsum(
        "gst,tgc->sgc", band_tile, grouped, preferred_element_type=jnp.float32
    ).reshape(row_count, channels)


def causal_taps(extended, weights, ext_ids, doc_ids):
    row_count = doc_ids.shape[0]
    summed = jnp.zeros((row_count, extended.shape[1]), jnp.float32)
    for offset in range(3):
        first_row = 2 - offset
        same_doc = ext_ids[first_row : first_row + row_count] == doc_ids
        summed = summed + jnp.where(
            same_doc[:, None],
            weights[offset][None, :]
            * extended[first_row : first_row + row_count].astype(jnp.float32),
            0.0,
        )
    return summed


def anti_taps(extended, weights, ext_ids, doc_ids):
    row_count = doc_ids.shape[0]
    summed = jnp.zeros((row_count, extended.shape[1]), jnp.float32)
    for offset in range(3):
        same_doc = ext_ids[offset : offset + row_count] == doc_ids
        summed = summed + jnp.where(
            same_doc[:, None],
            weights[offset][None, :] * extended[offset : offset + row_count].astype(jnp.float32),
            0.0,
        )
    return summed


def local(
    query_in,
    key_in,
    value_in,
    short_weight,
    long_filter,
    skip_weight,
    out_weight,
    doc_ids,
    out_grad,
):
    row_count, channels = query_in.shape
    before_ids = shifted(doc_ids[-2:] + 1, CTX, 1) - 1
    after_ids = shifted(doc_ids[:2] + 1, CTX, -1) - 1
    first_id = doc_ids[0]
    last_id = doc_ids[-1]
    prev_last = before_ids[1]
    next_first = after_ids[0]
    single_doc = first_id == last_id
    joins_next = next_first == last_id
    joins_prev = prev_last == first_id
    prev_rows = shifted((query_in[-2:], key_in[-2:], value_in[-2:]), CTX, 1)
    back_ids = jnp.concatenate([before_ids, doc_ids])
    query_short = causal_taps(
        jnp.concatenate([prev_rows[0], query_in]), short_weight[0], back_ids, doc_ids
    )
    key_short = causal_taps(
        jnp.concatenate([prev_rows[1], key_in]), short_weight[1], back_ids, doc_ids
    )
    value_short = causal_taps(
        jnp.concatenate([prev_rows[2], value_in]), short_weight[2], back_ids, doc_ids
    )
    gated = (key_short * value_short).astype(jnp.bfloat16)
    tiles_list = toeplitz_tiles(long_filter, row_count, HOPS)
    same_doc = doc_ids[:, None] == doc_ids[None, :]
    diagonal = jnp.where(same_doc[None], tiles_list[0], jnp.zeros((), tiles_list[0].dtype))
    head_rows = (doc_ids == first_id)[:, None]
    tail_rows = (doc_ids == last_id)[:, None]
    zero_half = jnp.zeros((), gated.dtype)

    def cross_term(is_live, product, band_tile, source):
        summand = jnp.where(is_live, product(band_tile, source), 0.0)
        return summand

    mixed = apply_forward(diagonal, gated) + skip_weight[None, :] * gated.astype(jnp.float32)
    own_tail = jnp.where(tail_rows, gated, zero_half)
    moving = jnp.where(joins_next, own_tail, zero_half)
    for distance in range(1, HOPS + 1):
        moving = shifted(moving, CTX, 1)
        is_live = jnp.any(moving != 0)
        mixed = mixed + jnp.where(
            head_rows, cross_term(is_live, apply_forward, tiles_list[distance], moving), 0.0
        )
        moving = jnp.where(single_doc & joins_next, moving, zero_half)
    pre_gate = (query_short * mixed).astype(jnp.bfloat16)
    pair_size = lax.axis_size("core")
    chip_count = lax.axis_size(CHIPS)
    weight_rows, weight_rows_other, core_index = gather_weight(out_weight, chip_count)
    ch_count = lax.axis_size(CH)
    spread = jnp.broadcast_to(pre_gate[None], (ch_count,) + pre_gate.shape)
    gathered = lax.all_to_all(spread, CH, 0, 0, tiled=True).reshape(
        ch_count, row_count, channels
    )
    full_pre = jnp.transpose(gathered, (1, 0, 2)).reshape(
        row_count, chip_count, pair_size, out_weight.shape[0]
    )
    pre_first = full_pre[:, :, 0].reshape(row_count, -1)
    pre_second = full_pre[:, :, 1].reshape(row_count, -1)
    on_first = core_index == 0
    pre_mine = jnp.where(on_first, pre_first, pre_second)
    pre_other = jnp.where(on_first, pre_second, pre_first)
    out_sum = jnp.dot(pre_mine, weight_rows, preferred_element_type=jnp.float32) + jnp.dot(
        pre_other, weight_rows_other, preferred_element_type=jnp.float32
    )
    dims = (((1,), (1,)), ((), ()))
    block_chips = chip_count // ch_count
    part_mine = lax.dot_general(
        weight_rows, out_grad, dims, preferred_element_type=jnp.float32
    ).reshape(ch_count, 1, block_chips, -1, row_count)
    part_other = lax.dot_general(
        weight_rows_other, out_grad, dims, preferred_element_type=jnp.float32
    ).reshape(ch_count, 1, block_chips, -1, row_count)
    sent = jnp.concatenate([part_mine, part_other], axis=1)
    summed = jnp.sum(lax.all_to_all(sent, CH, 0, 0, tiled=True), axis=0)
    cols_mine, cols_other = summed[0][:, None], summed[1][:, None]
    grad_cols = jnp.where(
        on_first,
        jnp.concatenate([cols_mine, cols_other], axis=1),
        jnp.concatenate([cols_other, cols_mine], axis=1),
    ).reshape(-1, row_count)
    layer_out = out_sum.astype(jnp.bfloat16)
    grad_pre = jnp.transpose(grad_cols)
    grad_query_short = (grad_pre * mixed).astype(jnp.bfloat16)
    grad_mixed = (grad_pre * query_short).astype(jnp.bfloat16)
    own_head = jnp.where(head_rows, grad_mixed, zero_half)
    grad_gated = apply_adjoint(diagonal, grad_mixed) + skip_weight[None, :] * grad_mixed.astype(
        jnp.float32
    )
    moving_back = jnp.where(joins_prev, own_head, zero_half)
    for distance in range(1, HOPS + 1):
        moving_back = shifted(moving_back, CTX, -1)
        is_live = jnp.any(moving_back != 0)
        grad_gated = grad_gated + jnp.where(
            tail_rows, cross_term(is_live, apply_adjoint, tiles_list[distance], moving_back), 0.0
        )
        moving_back = jnp.where(single_doc & joins_prev, moving_back, zero_half)
    grad_key_short = (grad_gated * value_short).astype(jnp.bfloat16)
    grad_value_short = (grad_gated * key_short).astype(jnp.bfloat16)
    next_rows = shifted((grad_query_short[:2], grad_key_short[:2], grad_value_short[:2]), CTX, -1)
    ahead_ids = jnp.concatenate([doc_ids, after_ids])
    grad_query = anti_taps(
        jnp.concatenate([grad_query_short, next_rows[0]]), short_weight[0], ahead_ids, doc_ids
    ).astype(jnp.bfloat16)
    grad_key = anti_taps(
        jnp.concatenate([grad_key_short, next_rows[1]]), short_weight[1], ahead_ids, doc_ids
    ).astype(jnp.bfloat16)
    grad_value = anti_taps(
        jnp.concatenate([grad_value_short, next_rows[2]]), short_weight[2], ahead_ids, doc_ids
    ).astype(jnp.bfloat16)
    return (layer_out, grad_query, grad_key, grad_value)


def solution(mesh):
    zl, y, core = 4, 8, 2
    split_mesh = Mesh(
        mesh.devices.reshape(zl, y, core, mesh.devices.shape[1] // 4, 4),
        ("zl", "y", "core", "zh", "x"),
    )
    return jax.shard_map(
        local,
        mesh=split_mesh,
        in_specs=(
            P(CTX, CH),
            P(CTX, CH),
            P(CTX, CH),
            P(None, None, CH),
            P(CH, None),
            P(CH),
            P(CTX, CH),
            P(CTX),
            P(CTX, CH),
        ),
        out_specs=(P(CTX, CH), P(CTX, CH), P(CTX, CH), P(CTX, CH)),
        check_vma=False,
    )
```

```python
import jax
import jax.numpy as jnp
from jax import lax
from jax.sharding import Mesh, PartitionSpec as P

HOPS = 3
CHIPS = ("zl", "y")
CTX = ("zl", "y", "core")
CH = ("zh", "x")


def gather_weight(out_weight, chip_count):
    spread = jnp.broadcast_to(out_weight[None], (chip_count,) + out_weight.shape)
    mine = lax.all_to_all(spread, CHIPS, 0, 0, tiled=True).reshape(-1, out_weight.shape[1])
    other = lax.ppermute(mine, "core", [(0, 1), (1, 0)])
    return mine, other, lax.axis_index("core")


def shifted(array, axis, by):
    size = lax.axis_size(axis)
    pairs = [(i, i + by) for i in range(size) if 0 <= i + by < size]
    return lax.ppermute(array, axis, pairs)


def toeplitz_tiles(long_filter, row_count, hop_count):
    group_count, span_len = long_filter.shape
    padded = jnp.concatenate(
        [
            jnp.zeros((group_count, row_count), long_filter.dtype),
            long_filter,
            jnp.zeros((group_count, (hop_count + 3) * row_count - span_len), long_filter.dtype),
        ],
        axis=1,
    )
    tiles_list = []
    for distance in range(hop_count + 1):
        window = padded[:, distance * row_count + 1 : distance * row_count + 1 + 2 * row_count]
        cyclic = jnp.concatenate(
            [
                window[:, row_count - 1 : 2 * row_count - 1],
                jnp.zeros((group_count, 1), window.dtype),
                window[:, : row_count - 1],
            ],
            axis=1,
        )
        repeated = jnp.tile(cyclic, (1, row_count))[:, : row_count * (2 * row_count - 1)]
        tiles_list.append(
            repeated.reshape(group_count, row_count, 2 * row_count - 1)[:, :, :row_count]
        )
    return tiles_list


def apply_forward(band_tile, source):
    row_count, channels = source.shape
    grouped = source.reshape(row_count, band_tile.shape[0], -1)
    return jnp.einsum(
        "gst,sgc->tgc", band_tile, grouped, preferred_element_type=jnp.float32
    ).reshape(row_count, channels)


def apply_adjoint(band_tile, source):
    row_count, channels = source.shape
    grouped = source.reshape(row_count, band_tile.shape[0], -1)
    return jnp.einsum(
        "gst,tgc->sgc", band_tile, grouped, preferred_element_type=jnp.float32
    ).reshape(row_count, channels)


def causal_taps(extended, weights, ext_ids, doc_ids):
    row_count = doc_ids.shape[0]
    summed = jnp.zeros((row_count, extended.shape[1]), jnp.float32)
    for offset in range(3):
        first_row = 2 - offset
        same_doc = ext_ids[first_row : first_row + row_count] == doc_ids
        summed = summed + jnp.where(
            same_doc[:, None],
            weights[offset][None, :]
            * extended[first_row : first_row + row_count].astype(jnp.float32),
            0.0,
        )
    return summed


def anti_taps(extended, weights, ext_ids, doc_ids):
    row_count = doc_ids.shape[0]
    summed = jnp.zeros((row_count, extended.shape[1]), jnp.float32)
    for offset in range(3):
        same_doc = ext_ids[offset : offset + row_count] == doc_ids
        summed = summed + jnp.where(
            same_doc[:, None],
            weights[offset][None, :] * extended[offset : offset + row_count].astype(jnp.float32),
            0.0,
        )
    return summed


def local(
    query_in,
    key_in,
    value_in,
    short_weight,
    long_filter,
    skip_weight,
    out_weight,
    doc_ids,
    out_grad,
):
    row_count, channels = query_in.shape
    before_ids = shifted(doc_ids[-2:] + 1, CTX, 1) - 1
    after_ids = shifted(doc_ids[:2] + 1, CTX, -1) - 1
    first_id = doc_ids[0]
    last_id = doc_ids[-1]
    prev_last = before_ids[1]
    next_first = after_ids[0]
    single_doc = first_id == last_id
    joins_next = next_first == last_id
    joins_prev = prev_last == first_id
    prev_rows = shifted((query_in[-2:], key_in[-2:], value_in[-2:]), CTX, 1)
    back_ids = jnp.concatenate([before_ids, doc_ids])
    query_short = causal_taps(
        jnp.concatenate([prev_rows[0], query_in]), short_weight[0], back_ids, doc_ids
    )
    key_short = causal_taps(
        jnp.concatenate([prev_rows[1], key_in]), short_weight[1], back_ids, doc_ids
    )
    value_short = causal_taps(
        jnp.concatenate([prev_rows[2], value_in]), short_weight[2], back_ids, doc_ids
    )
    gated = (key_short * value_short).astype(jnp.bfloat16)
    tiles_list = toeplitz_tiles(long_filter, row_count, HOPS)
    same_doc = doc_ids[:, None] == doc_ids[None, :]
    diagonal = jnp.where(same_doc[None], tiles_list[0], jnp.zeros((), tiles_list[0].dtype))
    head_rows = (doc_ids == first_id)[:, None]
    tail_rows = (doc_ids == last_id)[:, None]
    zero_half = jnp.zeros((), gated.dtype)

    def cross_term(is_live, product, band_tile, source):
        summand = jnp.where(is_live, product(band_tile, source), 0.0)
        return summand

    mixed = apply_forward(diagonal, gated) + skip_weight[None, :] * gated.astype(jnp.float32)
    own_tail = jnp.where(tail_rows, gated, zero_half)
    moving = jnp.where(joins_next, own_tail, zero_half)
    for distance in range(1, HOPS + 1):
        moving = shifted(moving, CTX, 1)
        is_live = jnp.any(moving != 0)
        mixed = mixed + jnp.where(
            head_rows, cross_term(is_live, apply_forward, tiles_list[distance], moving), 0.0
        )
        moving = jnp.where(single_doc & joins_next, moving, zero_half)
    pre_gate = (query_short * mixed).astype(jnp.bfloat16)
    pair_size = lax.axis_size("core")
    chip_count = lax.axis_size(CHIPS)
    weight_rows, weight_rows_other, core_index = gather_weight(out_weight, chip_count)
    ch_count = lax.axis_size(CH)
    spread = jnp.broadcast_to(pre_gate[None], (ch_count,) + pre_gate.shape)
    gathered = lax.all_to_all(spread, CH, 0, 0, tiled=True).reshape(
        ch_count, row_count, channels
    )
    full_pre = jnp.transpose(gathered, (1, 0, 2)).reshape(
        row_count, chip_count, pair_size, out_weight.shape[0]
    )
    pre_first = full_pre[:, :, 0].reshape(row_count, -1)
    pre_second = full_pre[:, :, 1].reshape(row_count, -1)
    on_first = core_index == 0
    pre_mine = jnp.where(on_first, pre_first, pre_second)
    pre_other = jnp.where(on_first, pre_second, pre_first)
    out_sum = jnp.dot(pre_mine, weight_rows, preferred_element_type=jnp.float32) + jnp.dot(
        pre_other, weight_rows_other, preferred_element_type=jnp.float32
    )
    dims = (((1,), (1,)), ((), ()))
    block_chips = chip_count // ch_count
    part_mine = lax.dot_general(
        weight_rows, out_grad, dims, preferred_element_type=jnp.float32
    ).reshape(ch_count, 1, block_chips, -1, row_count)
    part_other = lax.dot_general(
        weight_rows_other, out_grad, dims, preferred_element_type=jnp.float32
    ).reshape(ch_count, 1, block_chips, -1, row_count)
    sent = jnp.concatenate([part_mine, part_other], axis=1).astype(jnp.bfloat16)
    received = lax.all_to_all(sent, CH, 0, 0, tiled=True)
    summed = jnp.sum(received.astype(jnp.float32), axis=0)
    cols_mine, cols_other = summed[0][:, None], summed[1][:, None]
    grad_cols = jnp.where(
        on_first,
        jnp.concatenate([cols_mine, cols_other], axis=1),
        jnp.concatenate([cols_other, cols_mine], axis=1),
    ).reshape(-1, row_count)
    layer_out = out_sum.astype(jnp.bfloat16)
    grad_pre = jnp.transpose(grad_cols)
    grad_query_short = (grad_pre * mixed).astype(jnp.bfloat16)
    grad_mixed = (grad_pre * query_short).astype(jnp.bfloat16)
    own_head = jnp.where(head_rows, grad_mixed, zero_half)
    grad_gated = apply_adjoint(diagonal, grad_mixed) + skip_weight[None, :] * grad_mixed.astype(
        jnp.float32
    )
    moving_back = jnp.where(joins_prev, own_head, zero_half)
    for distance in range(1, HOPS + 1):
        moving_back = shifted(moving_back, CTX, -1)
        is_live = jnp.any(moving_back != 0)
        grad_gated = grad_gated + jnp.where(
            tail_rows, cross_term(is_live, apply_adjoint, tiles_list[distance], moving_back), 0.0
        )
        moving_back = jnp.where(single_doc & joins_prev, moving_back, zero_half)
    grad_key_short = (grad_gated * value_short).astype(jnp.bfloat16)
    grad_value_short = (grad_gated * key_short).astype(jnp.bfloat16)
    next_rows = shifted((grad_query_short[:2], grad_key_short[:2], grad_value_short[:2]), CTX, -1)
    ahead_ids = jnp.concatenate([doc_ids, after_ids])
    grad_query = anti_taps(
        jnp.concatenate([grad_query_short, next_rows[0]]), short_weight[0], ahead_ids, doc_ids
    ).astype(jnp.bfloat16)
    grad_key = anti_taps(
        jnp.concatenate([grad_key_short, next_rows[1]]), short_weight[1], ahead_ids, doc_ids
    ).astype(jnp.bfloat16)
    grad_value = anti_taps(
        jnp.concatenate([grad_value_short, next_rows[2]]), short_weight[2], ahead_ids, doc_ids
    ).astype(jnp.bfloat16)
    return (layer_out, grad_query, grad_key, grad_value)


def solution(mesh):
    zl, y, core = 4, 8, 2
    split_mesh = Mesh(
        mesh.devices.reshape(zl, y, core, mesh.devices.shape[1] // 4, 4),
        ("zl", "y", "core", "zh", "x"),
    )
    return jax.shard_map(
        local,
        mesh=split_mesh,
        in_specs=(
            P(CTX, CH),
            P(CTX, CH),
            P(CTX, CH),
            P(None, None, CH),
            P(CH, None),
            P(CH),
            P(CTX, CH),
            P(CTX),
            P(CTX, CH),
        ),
        out_specs=(P(CTX, CH), P(CTX, CH), P(CTX, CH), P(CTX, CH)),
        check_vma=False,
    )
```

```python
import jax
import jax.numpy as jnp
from jax import lax
from jax.sharding import Mesh, PartitionSpec as P

HOPS = 3
CHIPS = ("zl", "y")
CTX = ("zl", "y", "core")
CH = ("zh", "x")


def gather_along(block, axis):
    size = lax.axis_size(axis)
    parts = [block]
    for step in range(1, size):
        parts.append(lax.ppermute(block, axis, [(i, (i - step) % size) for i in range(size)]))
    return jnp.roll(jnp.stack(parts), lax.axis_index(axis), axis=0)


def gather_weight(out_weight, chip_count):
    along_y = gather_along(out_weight, "y")
    mine = gather_along(along_y, "zl").reshape(-1, out_weight.shape[1])
    other = lax.ppermute(mine, "core", [(0, 1), (1, 0)])
    return mine, other, lax.axis_index("core")


def shifted(array, axis, by):
    size = lax.axis_size(axis)
    pairs = [(i, i + by) for i in range(size) if 0 <= i + by < size]
    return lax.ppermute(array, axis, pairs)


def toeplitz_tiles(long_filter, row_count, hop_count):
    group_count, span_len = long_filter.shape
    padded = jnp.concatenate(
        [
            jnp.zeros((group_count, row_count), long_filter.dtype),
            long_filter,
            jnp.zeros((group_count, (hop_count + 3) * row_count - span_len), long_filter.dtype),
        ],
        axis=1,
    )
    tiles_list = []
    for distance in range(hop_count + 1):
        window = padded[:, distance * row_count + 1 : distance * row_count + 1 + 2 * row_count]
        cyclic = jnp.concatenate(
            [
                window[:, row_count - 1 : 2 * row_count - 1],
                jnp.zeros((group_count, 1), window.dtype),
                window[:, : row_count - 1],
            ],
            axis=1,
        )
        repeated = jnp.tile(cyclic, (1, row_count))[:, : row_count * (2 * row_count - 1)]
        tiles_list.append(
            repeated.reshape(group_count, row_count, 2 * row_count - 1)[:, :, :row_count]
        )
    return tiles_list


def apply_forward(band_tile, source):
    row_count, channels = source.shape
    grouped = source.reshape(row_count, band_tile.shape[0], -1)
    return jnp.einsum(
        "gst,sgc->tgc", band_tile, grouped, preferred_element_type=jnp.float32
    ).reshape(row_count, channels)


def apply_adjoint(band_tile, source):
    row_count, channels = source.shape
    grouped = source.reshape(row_count, band_tile.shape[0], -1)
    return jnp.einsum(
        "gst,tgc->sgc", band_tile, grouped, preferred_element_type=jnp.float32
    ).reshape(row_count, channels)


def causal_taps(extended, weights, ext_ids, doc_ids):
    row_count = doc_ids.shape[0]
    summed = jnp.zeros((row_count, extended.shape[1]), jnp.float32)
    for offset in range(3):
        first_row = 2 - offset
        same_doc = ext_ids[first_row : first_row + row_count] == doc_ids
        summed = summed + jnp.where(
            same_doc[:, None],
            weights[offset][None, :]
            * extended[first_row : first_row + row_count].astype(jnp.float32),
            0.0,
        )
    return summed


def anti_taps(extended, weights, ext_ids, doc_ids):
    row_count = doc_ids.shape[0]
    summed = jnp.zeros((row_count, extended.shape[1]), jnp.float32)
    for offset in range(3):
        same_doc = ext_ids[offset : offset + row_count] == doc_ids
        summed = summed + jnp.where(
            same_doc[:, None],
            weights[offset][None, :] * extended[offset : offset + row_count].astype(jnp.float32),
            0.0,
        )
    return summed


def local(
    query_in,
    key_in,
    value_in,
    short_weight,
    long_filter,
    skip_weight,
    out_weight,
    doc_ids,
    out_grad,
):
    row_count, channels = query_in.shape
    before_ids = shifted(doc_ids[-2:] + 1, CTX, 1) - 1
    after_ids = shifted(doc_ids[:2] + 1, CTX, -1) - 1
    first_id = doc_ids[0]
    last_id = doc_ids[-1]
    prev_last = before_ids[1]
    next_first = after_ids[0]
    single_doc = first_id == last_id
    joins_next = next_first == last_id
    joins_prev = prev_last == first_id
    prev_rows = shifted((query_in[-2:], key_in[-2:], value_in[-2:]), CTX, 1)
    back_ids = jnp.concatenate([before_ids, doc_ids])
    query_short = causal_taps(
        jnp.concatenate([prev_rows[0], query_in]), short_weight[0], back_ids, doc_ids
    )
    key_short = causal_taps(
        jnp.concatenate([prev_rows[1], key_in]), short_weight[1], back_ids, doc_ids
    )
    value_short = causal_taps(
        jnp.concatenate([prev_rows[2], value_in]), short_weight[2], back_ids, doc_ids
    )
    gated = (key_short * value_short).astype(jnp.bfloat16)
    tiles_list = toeplitz_tiles(long_filter, row_count, HOPS)
    same_doc = doc_ids[:, None] == doc_ids[None, :]
    diagonal = jnp.where(same_doc[None], tiles_list[0], jnp.zeros((), tiles_list[0].dtype))
    head_rows = (doc_ids == first_id)[:, None]
    tail_rows = (doc_ids == last_id)[:, None]
    zero_half = jnp.zeros((), gated.dtype)

    def cross_term(is_live, product, band_tile, source):
        summand = jnp.where(is_live, product(band_tile, source), 0.0)
        return summand

    mixed = apply_forward(diagonal, gated) + skip_weight[None, :] * gated.astype(jnp.float32)
    own_tail = jnp.where(tail_rows, gated, zero_half)
    moving = jnp.where(joins_next, own_tail, zero_half)
    for distance in range(1, HOPS + 1):
        moving = shifted(moving, CTX, 1)
        is_live = jnp.any(moving != 0)
        mixed = mixed + jnp.where(
            head_rows, cross_term(is_live, apply_forward, tiles_list[distance], moving), 0.0
        )
        moving = jnp.where(single_doc & joins_next, moving, zero_half)
    pre_gate = (query_short * mixed).astype(jnp.bfloat16)
    pair_size = lax.axis_size("core")
    chip_count = lax.axis_size(CHIPS)
    weight_rows, weight_rows_other, core_index = gather_weight(out_weight, chip_count)
    ch_count = lax.axis_size(CH)
    spread = jnp.broadcast_to(pre_gate[None], (ch_count,) + pre_gate.shape)
    gathered = lax.all_to_all(spread, CH, 0, 0, tiled=True).reshape(
        ch_count, row_count, channels
    )
    full_pre = jnp.transpose(gathered, (1, 0, 2)).reshape(
        row_count, chip_count, pair_size, out_weight.shape[0]
    )
    pre_first = full_pre[:, :, 0].reshape(row_count, -1)
    pre_second = full_pre[:, :, 1].reshape(row_count, -1)
    on_first = core_index == 0
    pre_mine = jnp.where(on_first, pre_first, pre_second)
    pre_other = jnp.where(on_first, pre_second, pre_first)
    out_sum = jnp.dot(pre_mine, weight_rows, preferred_element_type=jnp.float32) + jnp.dot(
        pre_other, weight_rows_other, preferred_element_type=jnp.float32
    )
    dims = (((1,), (1,)), ((), ()))
    block_chips = chip_count // ch_count
    part_mine = lax.dot_general(
        weight_rows, out_grad, dims, preferred_element_type=jnp.float32
    ).reshape(ch_count, 1, block_chips, -1, row_count)
    part_other = lax.dot_general(
        weight_rows_other, out_grad, dims, preferred_element_type=jnp.float32
    ).reshape(ch_count, 1, block_chips, -1, row_count)
    sent = jnp.concatenate([part_mine, part_other], axis=1)
    summed = jnp.sum(lax.all_to_all(sent, CH, 0, 0, tiled=True), axis=0)
    cols_mine, cols_other = summed[0][:, None], summed[1][:, None]
    grad_cols = jnp.where(
        on_first,
        jnp.concatenate([cols_mine, cols_other], axis=1),
        jnp.concatenate([cols_other, cols_mine], axis=1),
    ).reshape(-1, row_count)
    layer_out = out_sum.astype(jnp.bfloat16)
    grad_pre = jnp.transpose(grad_cols)
    grad_query_short = (grad_pre * mixed).astype(jnp.bfloat16)
    grad_mixed = (grad_pre * query_short).astype(jnp.bfloat16)
    own_head = jnp.where(head_rows, grad_mixed, zero_half)
    grad_gated = apply_adjoint(diagonal, grad_mixed) + skip_weight[None, :] * grad_mixed.astype(
        jnp.float32
    )
    moving_back = jnp.where(joins_prev, own_head, zero_half)
    for distance in range(1, HOPS + 1):
        moving_back = shifted(moving_back, CTX, -1)
        is_live = jnp.any(moving_back != 0)
        grad_gated = grad_gated + jnp.where(
            tail_rows, cross_term(is_live, apply_adjoint, tiles_list[distance], moving_back), 0.0
        )
        moving_back = jnp.where(single_doc & joins_prev, moving_back, zero_half)
    grad_key_short = (grad_gated * value_short).astype(jnp.bfloat16)
    grad_value_short = (grad_gated * key_short).astype(jnp.bfloat16)
    next_rows = shifted((grad_query_short[:2], grad_key_short[:2], grad_value_short[:2]), CTX, -1)
    ahead_ids = jnp.concatenate([doc_ids, after_ids])
    grad_query = anti_taps(
        jnp.concatenate([grad_query_short, next_rows[0]]), short_weight[0], ahead_ids, doc_ids
    ).astype(jnp.bfloat16)
    grad_key = anti_taps(
        jnp.concatenate([grad_key_short, next_rows[1]]), short_weight[1], ahead_ids, doc_ids
    ).astype(jnp.bfloat16)
    grad_value = anti_taps(
        jnp.concatenate([grad_value_short, next_rows[2]]), short_weight[2], ahead_ids, doc_ids
    ).astype(jnp.bfloat16)
    return (layer_out, grad_query, grad_key, grad_value)


def solution(mesh):
    zl, y, core = 4, 8, 2
    split_mesh = Mesh(
        mesh.devices.reshape(zl, y, core, mesh.devices.shape[1] // 4, 4),
        ("zl", "y", "core", "zh", "x"),
    )
    return jax.shard_map(
        local,
        mesh=split_mesh,
        in_specs=(
            P(CTX, CH),
            P(CTX, CH),
            P(CTX, CH),
            P(None, None, CH),
            P(CH, None),
            P(CH),
            P(CTX, CH),
            P(CTX),
            P(CTX, CH),
        ),
        out_specs=(P(CTX, CH), P(CTX, CH), P(CTX, CH), P(CTX, CH)),
        check_vma=False,
    )
```

```python
import jax
import jax.numpy as jnp
from jax import lax
from jax.sharding import Mesh, PartitionSpec as P

HOPS = 3
CHIPS = ("zl", "y")
CTX = ("zl", "y", "core")
CH = ("zh", "x")


def gather_weight(out_weight, chip_count):
    spread = jnp.broadcast_to(out_weight[None], (chip_count,) + out_weight.shape)
    mine = lax.all_to_all(spread, CHIPS, 0, 0, tiled=True).reshape(-1, out_weight.shape[1])
    other = lax.ppermute(mine, "core", [(0, 1), (1, 0)])
    return mine, other, lax.axis_index("core")


def shifted(array, axis, by):
    size = lax.axis_size(axis)
    pairs = [(i, i + by) for i in range(size) if 0 <= i + by < size]
    return lax.ppermute(array, axis, pairs)


def toeplitz_tiles(long_filter, row_count, hop_count):
    group_count, span_len = long_filter.shape
    padded = jnp.concatenate(
        [
            jnp.zeros((group_count, row_count), long_filter.dtype),
            long_filter,
            jnp.zeros((group_count, (hop_count + 3) * row_count - span_len), long_filter.dtype),
        ],
        axis=1,
    )
    tiles_list = []
    for distance in range(hop_count + 1):
        window = padded[:, distance * row_count + 1 : distance * row_count + 1 + 2 * row_count]
        cyclic = jnp.concatenate(
            [
                window[:, row_count - 1 : 2 * row_count - 1],
                jnp.zeros((group_count, 1), window.dtype),
                window[:, : row_count - 1],
            ],
            axis=1,
        )
        repeated = jnp.tile(cyclic, (1, row_count))[:, : row_count * (2 * row_count - 1)]
        tiles_list.append(
            repeated.reshape(group_count, row_count, 2 * row_count - 1)[:, :, :row_count]
        )
    return tiles_list


def apply_forward(band_tile, source):
    row_count, channels = source.shape
    grouped = source.reshape(row_count, band_tile.shape[0], -1)
    return jnp.einsum(
        "gst,sgc->tgc", band_tile, grouped, preferred_element_type=jnp.float32
    ).reshape(row_count, channels)


def apply_adjoint(band_tile, source):
    row_count, channels = source.shape
    grouped = source.reshape(row_count, band_tile.shape[0], -1)
    return jnp.einsum(
        "gst,tgc->sgc", band_tile, grouped, preferred_element_type=jnp.float32
    ).reshape(row_count, channels)


def causal_taps(extended, weights, ext_ids, doc_ids):
    row_count = doc_ids.shape[0]
    summed = jnp.zeros((row_count, extended.shape[1]), jnp.float32)
    for offset in range(3):
        first_row = 2 - offset
        same_doc = ext_ids[first_row : first_row + row_count] == doc_ids
        summed = summed + jnp.where(
            same_doc[:, None],
            weights[offset][None, :]
            * extended[first_row : first_row + row_count].astype(jnp.float32),
            0.0,
        )
    return summed


def anti_taps(extended, weights, ext_ids, doc_ids):
    row_count = doc_ids.shape[0]
    summed = jnp.zeros((row_count, extended.shape[1]), jnp.float32)
    for offset in range(3):
        same_doc = ext_ids[offset : offset + row_count] == doc_ids
        summed = summed + jnp.where(
            same_doc[:, None],
            weights[offset][None, :] * extended[offset : offset + row_count].astype(jnp.float32),
            0.0,
        )
    return summed


def local(
    query_in,
    key_in,
    value_in,
    short_weight,
    long_filter,
    skip_weight,
    out_weight,
    doc_ids,
    out_grad,
):
    row_count, channels = query_in.shape
    before_ids = shifted(doc_ids[-2:] + 1, CTX, 1) - 1
    after_ids = shifted(doc_ids[:2] + 1, CTX, -1) - 1
    first_id = doc_ids[0]
    last_id = doc_ids[-1]
    prev_last = before_ids[1]
    next_first = after_ids[0]
    single_doc = first_id == last_id
    joins_next = next_first == last_id
    joins_prev = prev_last == first_id
    prev_rows = shifted((query_in[-2:], key_in[-2:], value_in[-2:]), CTX, 1)
    back_ids = jnp.concatenate([before_ids, doc_ids])
    query_short = causal_taps(
        jnp.concatenate([prev_rows[0], query_in]), short_weight[0], back_ids, doc_ids
    )
    key_short = causal_taps(
        jnp.concatenate([prev_rows[1], key_in]), short_weight[1], back_ids, doc_ids
    )
    value_short = causal_taps(
        jnp.concatenate([prev_rows[2], value_in]), short_weight[2], back_ids, doc_ids
    )
    gated = (key_short * value_short).astype(jnp.bfloat16)
    tiles_list = toeplitz_tiles(long_filter, row_count, HOPS)
    same_doc = doc_ids[:, None] == doc_ids[None, :]
    diagonal = jnp.where(same_doc[None], tiles_list[0], jnp.zeros((), tiles_list[0].dtype))
    head_rows = (doc_ids == first_id)[:, None]
    tail_rows = (doc_ids == last_id)[:, None]
    zero_half = jnp.zeros((), gated.dtype)

    def cross_term(is_live, product, band_tile, source):
        summand = jnp.where(is_live, product(band_tile, source), 0.0)
        return summand

    mixed = apply_forward(diagonal, gated) + skip_weight[None, :] * gated.astype(jnp.float32)
    own_tail = jnp.where(tail_rows, gated, zero_half)
    moving = jnp.where(joins_next, own_tail, zero_half)
    for distance in range(1, HOPS + 1):
        moving = shifted(moving, CTX, 1)
        is_live = jnp.any(moving != 0)
        mixed = mixed + jnp.where(
            head_rows, cross_term(is_live, apply_forward, tiles_list[distance], moving), 0.0
        )
        moving = jnp.where(single_doc & joins_next, moving, zero_half)
    pre_gate = (query_short * mixed).astype(jnp.bfloat16)
    pair_size = lax.axis_size("core")
    chip_count = lax.axis_size(CHIPS)
    weight_rows, weight_rows_other, core_index = gather_weight(out_weight, chip_count)
    ch_count = lax.axis_size(CH)
    far_count = lax.axis_size("zh")
    near_count = lax.axis_size("x")
    paired = lax.all_to_all(
        jnp.broadcast_to(pre_gate[None], (far_count,) + pre_gate.shape), "zh", 0, 0, tiled=True
    )
    gathered = lax.all_to_all(
        jnp.broadcast_to(paired[None], (near_count,) + paired.shape), "x", 0, 0, tiled=True
    )
    gathered = jnp.transpose(gathered, (1, 0, 2, 3)).reshape(ch_count, row_count, channels)
    full_pre = jnp.transpose(gathered, (1, 0, 2)).reshape(
        row_count, chip_count, pair_size, out_weight.shape[0]
    )
    pre_first = full_pre[:, :, 0].reshape(row_count, -1)
    pre_second = full_pre[:, :, 1].reshape(row_count, -1)
    on_first = core_index == 0
    pre_mine = jnp.where(on_first, pre_first, pre_second)
    pre_other = jnp.where(on_first, pre_second, pre_first)
    out_sum = jnp.dot(pre_mine, weight_rows, preferred_element_type=jnp.float32) + jnp.dot(
        pre_other, weight_rows_other, preferred_element_type=jnp.float32
    )
    dims = (((1,), (1,)), ((), ()))
    block_chips = chip_count // ch_count
    part_mine = lax.dot_general(
        weight_rows, out_grad, dims, preferred_element_type=jnp.float32
    ).reshape(ch_count, 1, block_chips, -1, row_count)
    part_other = lax.dot_general(
        weight_rows_other, out_grad, dims, preferred_element_type=jnp.float32
    ).reshape(ch_count, 1, block_chips, -1, row_count)
    sent = jnp.concatenate([part_mine, part_other], axis=1).reshape(
        far_count, near_count, 2, block_chips, -1, row_count
    )
    near_sum = jnp.sum(lax.all_to_all(sent, "x", 1, 1, tiled=True), axis=1)
    summed = jnp.sum(lax.all_to_all(near_sum, "zh", 0, 0, tiled=True), axis=0)
    cols_mine, cols_other = summed[0][:, None], summed[1][:, None]
    grad_cols = jnp.where(
        on_first,
        jnp.concatenate([cols_mine, cols_other], axis=1),
        jnp.concatenate([cols_other, cols_mine], axis=1),
    ).reshape(-1, row_count)
    layer_out = out_sum.astype(jnp.bfloat16)
    grad_pre = jnp.transpose(grad_cols)
    grad_query_short = (grad_pre * mixed).astype(jnp.bfloat16)
    grad_mixed = (grad_pre * query_short).astype(jnp.bfloat16)
    own_head = jnp.where(head_rows, grad_mixed, zero_half)
    grad_gated = apply_adjoint(diagonal, grad_mixed) + skip_weight[None, :] * grad_mixed.astype(
        jnp.float32
    )
    moving_back = jnp.where(joins_prev, own_head, zero_half)
    for distance in range(1, HOPS + 1):
        moving_back = shifted(moving_back, CTX, -1)
        is_live = jnp.any(moving_back != 0)
        grad_gated = grad_gated + jnp.where(
            tail_rows, cross_term(is_live, apply_adjoint, tiles_list[distance], moving_back), 0.0
        )
        moving_back = jnp.where(single_doc & joins_prev, moving_back, zero_half)
    grad_key_short = (grad_gated * value_short).astype(jnp.bfloat16)
    grad_value_short = (grad_gated * key_short).astype(jnp.bfloat16)
    next_rows = shifted((grad_query_short[:2], grad_key_short[:2], grad_value_short[:2]), CTX, -1)
    ahead_ids = jnp.concatenate([doc_ids, after_ids])
    grad_query = anti_taps(
        jnp.concatenate([grad_query_short, next_rows[0]]), short_weight[0], ahead_ids, doc_ids
    ).astype(jnp.bfloat16)
    grad_key = anti_taps(
        jnp.concatenate([grad_key_short, next_rows[1]]), short_weight[1], ahead_ids, doc_ids
    ).astype(jnp.bfloat16)
    grad_value = anti_taps(
        jnp.concatenate([grad_value_short, next_rows[2]]), short_weight[2], ahead_ids, doc_ids
    ).astype(jnp.bfloat16)
    return (layer_out, grad_query, grad_key, grad_value)


def solution(mesh):
    zl, y, core = 4, 8, 2
    split_mesh = Mesh(
        mesh.devices.reshape(zl, y, core, mesh.devices.shape[1] // 4, 4),
        ("zl", "y", "core", "zh", "x"),
    )
    return jax.shard_map(
        local,
        mesh=split_mesh,
        in_specs=(
            P(CTX, CH),
            P(CTX, CH),
            P(CTX, CH),
            P(None, None, CH),
            P(CH, None),
            P(CH),
            P(CTX, CH),
            P(CTX),
            P(CTX, CH),
        ),
        out_specs=(P(CTX, CH), P(CTX, CH), P(CTX, CH), P(CTX, CH)),
        check_vma=False,
    )
```

```python
import jax
import jax.numpy as jnp
from jax import lax
from jax.sharding import Mesh, PartitionSpec as P

HOPS = 3
CHIPS = ("zl", "y")
CTX = ("zl", "y", "core")
CH = ("zh", "x")


def gather_weight(out_weight, chip_count):
    spread = jnp.broadcast_to(out_weight[None], (chip_count,) + out_weight.shape)
    mine = lax.all_to_all(spread, CHIPS, 0, 0, tiled=True).reshape(-1, out_weight.shape[1])
    other = lax.ppermute(mine, "core", [(0, 1), (1, 0)])
    return mine, other, lax.axis_index("core")


def shifted(array, axis, by):
    size = lax.axis_size(axis)
    pairs = [(i, i + by) for i in range(size) if 0 <= i + by < size]
    return lax.ppermute(array, axis, pairs)


def toeplitz_tiles(long_filter, row_count, hop_count):
    group_count, span_len = long_filter.shape
    padded = jnp.concatenate(
        [
            jnp.zeros((group_count, row_count), long_filter.dtype),
            long_filter,
            jnp.zeros((group_count, (hop_count + 3) * row_count - span_len), long_filter.dtype),
        ],
        axis=1,
    )
    tiles_list = []
    for distance in range(hop_count + 1):
        window = padded[:, distance * row_count + 1 : distance * row_count + 1 + 2 * row_count]
        cyclic = jnp.concatenate(
            [
                window[:, row_count - 1 : 2 * row_count - 1],
                jnp.zeros((group_count, 1), window.dtype),
                window[:, : row_count - 1],
            ],
            axis=1,
        )
        repeated = jnp.tile(cyclic, (1, row_count))[:, : row_count * (2 * row_count - 1)]
        tiles_list.append(
            repeated.reshape(group_count, row_count, 2 * row_count - 1)[:, :, :row_count]
        )
    return tiles_list


def apply_forward(band_tile, source):
    row_count, channels = source.shape
    grouped = source.reshape(row_count, band_tile.shape[0], -1)
    return jnp.einsum(
        "gst,sgc->tgc", band_tile, grouped, preferred_element_type=jnp.float32
    ).reshape(row_count, channels)


def apply_adjoint(band_tile, source):
    row_count, channels = source.shape
    grouped = source.reshape(row_count, band_tile.shape[0], -1)
    return jnp.einsum(
        "gst,tgc->sgc", band_tile, grouped, preferred_element_type=jnp.float32
    ).reshape(row_count, channels)


def causal_taps(extended, weights, ext_ids, doc_ids):
    row_count = doc_ids.shape[0]
    summed = jnp.zeros((row_count, extended.shape[1]), jnp.float32)
    for offset in range(3):
        first_row = 2 - offset
        same_doc = ext_ids[first_row : first_row + row_count] == doc_ids
        summed = summed + jnp.where(
            same_doc[:, None],
            weights[offset][None, :]
            * extended[first_row : first_row + row_count].astype(jnp.float32),
            0.0,
        )
    return summed


def anti_taps(extended, weights, ext_ids, doc_ids):
    row_count = doc_ids.shape[0]
    summed = jnp.zeros((row_count, extended.shape[1]), jnp.float32)
    for offset in range(3):
        same_doc = ext_ids[offset : offset + row_count] == doc_ids
        summed = summed + jnp.where(
            same_doc[:, None],
            weights[offset][None, :] * extended[offset : offset + row_count].astype(jnp.float32),
            0.0,
        )
    return summed


def local(
    query_in,
    key_in,
    value_in,
    short_weight,
    long_filter,
    skip_weight,
    out_weight,
    doc_ids,
    out_grad,
):
    row_count, channels = query_in.shape
    before_ids = shifted(doc_ids[-2:] + 1, CTX, 1) - 1
    after_ids = shifted(doc_ids[:2] + 1, CTX, -1) - 1
    first_id = doc_ids[0]
    last_id = doc_ids[-1]
    prev_last = before_ids[1]
    next_first = after_ids[0]
    single_doc = first_id == last_id
    joins_next = next_first == last_id
    joins_prev = prev_last == first_id
    prev_rows = shifted((query_in[-2:], key_in[-2:], value_in[-2:]), CTX, 1)
    back_ids = jnp.concatenate([before_ids, doc_ids])
    query_short = causal_taps(
        jnp.concatenate([prev_rows[0], query_in]), short_weight[0], back_ids, doc_ids
    )
    key_short = causal_taps(
        jnp.concatenate([prev_rows[1], key_in]), short_weight[1], back_ids, doc_ids
    )
    value_short = causal_taps(
        jnp.concatenate([prev_rows[2], value_in]), short_weight[2], back_ids, doc_ids
    )
    gated = (key_short * value_short).astype(jnp.bfloat16)
    tiles_list = toeplitz_tiles(long_filter, row_count, HOPS)
    same_doc = doc_ids[:, None] == doc_ids[None, :]
    diagonal = jnp.where(same_doc[None], tiles_list[0], jnp.zeros((), tiles_list[0].dtype))
    head_rows = (doc_ids == first_id)[:, None]
    tail_rows = (doc_ids == last_id)[:, None]
    zero_half = jnp.zeros((), gated.dtype)

    def cross_term(is_live, product, band_tile, source):
        summand = jnp.where(is_live, product(band_tile, source), 0.0)
        return summand

    mixed = apply_forward(diagonal, gated) + skip_weight[None, :] * gated.astype(jnp.float32)
    own_tail = jnp.where(tail_rows, gated, zero_half)
    moving = jnp.where(joins_next, own_tail, zero_half)
    for distance in range(1, HOPS + 1):
        moving = shifted(moving, CTX, 1)
        is_live = jnp.any(moving != 0)
        mixed = mixed + jnp.where(
            head_rows, cross_term(is_live, apply_forward, tiles_list[distance], moving), 0.0
        )
        moving = jnp.where(single_doc & joins_next, moving, zero_half)
    pre_gate = (query_short * mixed).astype(jnp.bfloat16)
    pair_size = lax.axis_size("core")
    chip_count = lax.axis_size(CHIPS)
    weight_rows, weight_rows_other, core_index = gather_weight(out_weight, chip_count)
    ch_count = lax.axis_size(CH)
    spread = jnp.broadcast_to(pre_gate[None], (ch_count,) + pre_gate.shape)
    gathered = lax.all_to_all(spread, CH, 0, 0, tiled=True).reshape(
        ch_count, row_count, channels
    )
    full_pre = jnp.transpose(gathered, (1, 0, 2)).reshape(
        row_count, chip_count, pair_size, out_weight.shape[0]
    )
    pre_first = full_pre[:, :, 0].reshape(row_count, -1)
    pre_second = full_pre[:, :, 1].reshape(row_count, -1)
    on_first = core_index == 0
    pre_mine = jnp.where(on_first, pre_first, pre_second)
    pre_other = jnp.where(on_first, pre_second, pre_first)
    out_sum = jnp.dot(pre_mine, weight_rows, preferred_element_type=jnp.float32) + jnp.dot(
        pre_other, weight_rows_other, preferred_element_type=jnp.float32
    )
    dims = (((1,), (1,)), ((), ()))
    block_chips = chip_count // ch_count

    def summed_over_ch(weight_half):
        part = lax.dot_general(weight_half, out_grad, dims, preferred_element_type=jnp.float32)
        received = lax.all_to_all(
            part.reshape(ch_count, block_chips, -1, row_count), CH, 0, 0, tiled=True
        )
        return jnp.sum(received, axis=0)

    summed = (summed_over_ch(weight_rows), summed_over_ch(weight_rows_other))
    cols_mine, cols_other = summed[0][:, None], summed[1][:, None]
    grad_cols = jnp.where(
        on_first,
        jnp.concatenate([cols_mine, cols_other], axis=1),
        jnp.concatenate([cols_other, cols_mine], axis=1),
    ).reshape(-1, row_count)
    layer_out = out_sum.astype(jnp.bfloat16)
    grad_pre = jnp.transpose(grad_cols)
    grad_query_short = (grad_pre * mixed).astype(jnp.bfloat16)
    grad_mixed = (grad_pre * query_short).astype(jnp.bfloat16)
    own_head = jnp.where(head_rows, grad_mixed, zero_half)
    grad_gated = apply_adjoint(diagonal, grad_mixed) + skip_weight[None, :] * grad_mixed.astype(
        jnp.float32
    )
    moving_back = jnp.where(joins_prev, own_head, zero_half)
    for distance in range(1, HOPS + 1):
        moving_back = shifted(moving_back, CTX, -1)
        is_live = jnp.any(moving_back != 0)
        grad_gated = grad_gated + jnp.where(
            tail_rows, cross_term(is_live, apply_adjoint, tiles_list[distance], moving_back), 0.0
        )
        moving_back = jnp.where(single_doc & joins_prev, moving_back, zero_half)
    grad_key_short = (grad_gated * value_short).astype(jnp.bfloat16)
    grad_value_short = (grad_gated * key_short).astype(jnp.bfloat16)
    next_rows = shifted((grad_query_short[:2], grad_key_short[:2], grad_value_short[:2]), CTX, -1)
    ahead_ids = jnp.concatenate([doc_ids, after_ids])
    grad_query = anti_taps(
        jnp.concatenate([grad_query_short, next_rows[0]]), short_weight[0], ahead_ids, doc_ids
    ).astype(jnp.bfloat16)
    grad_key = anti_taps(
        jnp.concatenate([grad_key_short, next_rows[1]]), short_weight[1], ahead_ids, doc_ids
    ).astype(jnp.bfloat16)
    grad_value = anti_taps(
        jnp.concatenate([grad_value_short, next_rows[2]]), short_weight[2], ahead_ids, doc_ids
    ).astype(jnp.bfloat16)
    return (layer_out, grad_query, grad_key, grad_value)


def solution(mesh):
    zl, y, core = 4, 8, 2
    split_mesh = Mesh(
        mesh.devices.reshape(zl, y, core, mesh.devices.shape[1] // 4, 4),
        ("zl", "y", "core", "zh", "x"),
    )
    return jax.shard_map(
        local,
        mesh=split_mesh,
        in_specs=(
            P(CTX, CH),
            P(CTX, CH),
            P(CTX, CH),
            P(None, None, CH),
            P(CH, None),
            P(CH),
            P(CTX, CH),
            P(CTX),
            P(CTX, CH),
        ),
        out_specs=(P(CTX, CH), P(CTX, CH), P(CTX, CH), P(CTX, CH)),
        check_vma=False,
    )
```

```python
import jax
import jax.numpy as jnp
from jax import lax
from jax.sharding import Mesh, PartitionSpec as P

HOPS = 3
CHIPS = ("zl", "y")
CTX = ("zl", "y", "core")
CH = ("zh", "x")


def gather_weight(out_weight, chip_count):
    spread = jnp.broadcast_to(out_weight[None], (chip_count,) + out_weight.shape)
    mine = lax.all_to_all(spread, CHIPS, 0, 0, tiled=True).reshape(-1, out_weight.shape[1])
    other = lax.ppermute(mine, "core", [(0, 1), (1, 0)])
    return mine, other, lax.axis_index("core")


def shifted(array, axis, by):
    size = lax.axis_size(axis)
    pairs = [(i, i + by) for i in range(size) if 0 <= i + by < size]
    return lax.ppermute(array, axis, pairs)


def toeplitz_tiles(long_filter, row_count, hop_count):
    group_count, span_len = long_filter.shape
    padded = jnp.concatenate(
        [
            jnp.zeros((group_count, row_count), long_filter.dtype),
            long_filter,
            jnp.zeros((group_count, (hop_count + 3) * row_count - span_len), long_filter.dtype),
        ],
        axis=1,
    )
    tiles_list = []
    for distance in range(hop_count + 1):
        window = padded[:, distance * row_count + 1 : distance * row_count + 1 + 2 * row_count]
        cyclic = jnp.concatenate(
            [
                window[:, row_count - 1 : 2 * row_count - 1],
                jnp.zeros((group_count, 1), window.dtype),
                window[:, : row_count - 1],
            ],
            axis=1,
        )
        repeated = jnp.tile(cyclic, (1, row_count))[:, : row_count * (2 * row_count - 1)]
        tiles_list.append(
            repeated.reshape(group_count, row_count, 2 * row_count - 1)[:, :, :row_count]
        )
    return tiles_list


def apply_forward(band_tile, source):
    row_count, channels = source.shape
    grouped = source.reshape(row_count, band_tile.shape[0], -1)
    return jnp.einsum(
        "gst,sgc->tgc", band_tile, grouped, preferred_element_type=jnp.float32
    ).reshape(row_count, channels)


def apply_adjoint(band_tile, source):
    row_count, channels = source.shape
    grouped = source.reshape(row_count, band_tile.shape[0], -1)
    return jnp.einsum(
        "gst,tgc->sgc", band_tile, grouped, preferred_element_type=jnp.float32
    ).reshape(row_count, channels)


def tagged(rows, doc_id):
    tag = jnp.full((1, rows.shape[1]), doc_id + 1, rows.dtype)
    return jnp.concatenate([rows, tag])


def untagged(block):
    return block[:-1], block[-1, 0].astype(jnp.int32) - 1


def causal_taps(extended, weights, ext_ids, doc_ids):
    row_count = doc_ids.shape[0]
    summed = jnp.zeros((row_count, extended.shape[1]), jnp.float32)
    for offset in range(3):
        first_row = 2 - offset
        same_doc = ext_ids[first_row : first_row + row_count] == doc_ids
        summed = summed + jnp.where(
            same_doc[:, None],
            weights[offset][None, :]
            * extended[first_row : first_row + row_count].astype(jnp.float32),
            0.0,
        )
    return summed


def anti_taps(extended, weights, ext_ids, doc_ids):
    row_count = doc_ids.shape[0]
    summed = jnp.zeros((row_count, extended.shape[1]), jnp.float32)
    for offset in range(3):
        same_doc = ext_ids[offset : offset + row_count] == doc_ids
        summed = summed + jnp.where(
            same_doc[:, None],
            weights[offset][None, :] * extended[offset : offset + row_count].astype(jnp.float32),
            0.0,
        )
    return summed


def local(
    query_in,
    key_in,
    value_in,
    short_weight,
    long_filter,
    skip_weight,
    out_weight,
    doc_ids,
    out_grad,
):
    row_count, channels = query_in.shape
    before_ids = shifted(doc_ids[-2:] + 1, CTX, 1) - 1
    after_ids = shifted(doc_ids[:2] + 1, CTX, -1) - 1
    first_id = doc_ids[0]
    last_id = doc_ids[-1]
    prev_last = before_ids[1]
    next_first = after_ids[0]
    single_doc = first_id == last_id
    joins_next = next_first == last_id
    joins_prev = prev_last == first_id
    prev_rows = shifted((query_in[-2:], key_in[-2:], value_in[-2:]), CTX, 1)
    back_ids = jnp.concatenate([before_ids, doc_ids])
    query_short = causal_taps(
        jnp.concatenate([prev_rows[0], query_in]), short_weight[0], back_ids, doc_ids
    )
    key_short = causal_taps(
        jnp.concatenate([prev_rows[1], key_in]), short_weight[1], back_ids, doc_ids
    )
    value_short = causal_taps(
        jnp.concatenate([prev_rows[2], value_in]), short_weight[2], back_ids, doc_ids
    )
    gated = (key_short * value_short).astype(jnp.bfloat16)
    tiles_list = toeplitz_tiles(long_filter, row_count, HOPS)
    same_doc = doc_ids[:, None] == doc_ids[None, :]
    diagonal = jnp.where(same_doc[None], tiles_list[0], jnp.zeros((), tiles_list[0].dtype))
    head_rows = (doc_ids == first_id)[:, None]
    tail_rows = (doc_ids == last_id)[:, None]
    zero_half = jnp.zeros((), gated.dtype)

    def cross_term(is_live, product, band_tile, source):
        summand = jnp.where(is_live, product(band_tile, source), 0.0)
        return summand

    mixed = apply_forward(diagonal, gated) + skip_weight[None, :] * gated.astype(jnp.float32)
    own_tail = tagged(jnp.where(tail_rows, gated, zero_half), last_id)
    for distance in range(1, HOPS + 1):
        moving, source_id = untagged(shifted(own_tail, CTX, distance))
        mixed = mixed + jnp.where(
            head_rows & (source_id == first_id),
            apply_forward(tiles_list[distance], moving),
            0.0,
        )
    pre_gate = (query_short * mixed).astype(jnp.bfloat16)
    pair_size = lax.axis_size("core")
    chip_count = lax.axis_size(CHIPS)
    weight_rows, weight_rows_other, core_index = gather_weight(out_weight, chip_count)
    ch_count = lax.axis_size(CH)
    spread = jnp.broadcast_to(pre_gate[None], (ch_count,) + pre_gate.shape)
    gathered = lax.all_to_all(spread, CH, 0, 0, tiled=True).reshape(
        ch_count, row_count, channels
    )
    full_pre = jnp.transpose(gathered, (1, 0, 2)).reshape(
        row_count, chip_count, pair_size, out_weight.shape[0]
    )
    pre_first = full_pre[:, :, 0].reshape(row_count, -1)
    pre_second = full_pre[:, :, 1].reshape(row_count, -1)
    on_first = core_index == 0
    pre_mine = jnp.where(on_first, pre_first, pre_second)
    pre_other = jnp.where(on_first, pre_second, pre_first)
    out_sum = jnp.dot(pre_mine, weight_rows, preferred_element_type=jnp.float32) + jnp.dot(
        pre_other, weight_rows_other, preferred_element_type=jnp.float32
    )
    dims = (((1,), (1,)), ((), ()))
    block_chips = chip_count // ch_count
    part_mine = lax.dot_general(
        weight_rows, out_grad, dims, preferred_element_type=jnp.float32
    ).reshape(ch_count, 1, block_chips, -1, row_count)
    part_other = lax.dot_general(
        weight_rows_other, out_grad, dims, preferred_element_type=jnp.float32
    ).reshape(ch_count, 1, block_chips, -1, row_count)
    sent = jnp.concatenate([part_mine, part_other], axis=1)
    summed = jnp.sum(lax.all_to_all(sent, CH, 0, 0, tiled=True), axis=0)
    cols_mine, cols_other = summed[0][:, None], summed[1][:, None]
    grad_cols = jnp.where(
        on_first,
        jnp.concatenate([cols_mine, cols_other], axis=1),
        jnp.concatenate([cols_other, cols_mine], axis=1),
    ).reshape(-1, row_count)
    layer_out = out_sum.astype(jnp.bfloat16)
    grad_pre = jnp.transpose(grad_cols)
    grad_query_short = (grad_pre * mixed).astype(jnp.bfloat16)
    grad_mixed = (grad_pre * query_short).astype(jnp.bfloat16)
    own_head = jnp.where(head_rows, grad_mixed, zero_half)
    grad_gated = apply_adjoint(diagonal, grad_mixed) + skip_weight[None, :] * grad_mixed.astype(
        jnp.float32
    )
    own_head = tagged(own_head, first_id)
    for distance in range(1, HOPS + 1):
        moving_back, source_id = untagged(shifted(own_head, CTX, -distance))
        grad_gated = grad_gated + jnp.where(
            tail_rows & (source_id == last_id),
            apply_adjoint(tiles_list[distance], moving_back),
            0.0,
        )
    grad_key_short = (grad_gated * value_short).astype(jnp.bfloat16)
    grad_value_short = (grad_gated * key_short).astype(jnp.bfloat16)
    next_rows = shifted((grad_query_short[:2], grad_key_short[:2], grad_value_short[:2]), CTX, -1)
    ahead_ids = jnp.concatenate([doc_ids, after_ids])
    grad_query = anti_taps(
        jnp.concatenate([grad_query_short, next_rows[0]]), short_weight[0], ahead_ids, doc_ids
    ).astype(jnp.bfloat16)
    grad_key = anti_taps(
        jnp.concatenate([grad_key_short, next_rows[1]]), short_weight[1], ahead_ids, doc_ids
    ).astype(jnp.bfloat16)
    grad_value = anti_taps(
        jnp.concatenate([grad_value_short, next_rows[2]]), short_weight[2], ahead_ids, doc_ids
    ).astype(jnp.bfloat16)
    return (layer_out, grad_query, grad_key, grad_value)


def solution(mesh):
    zl, y, core = 4, 8, 2
    split_mesh = Mesh(
        mesh.devices.reshape(zl, y, core, mesh.devices.shape[1] // 4, 4),
        ("zl", "y", "core", "zh", "x"),
    )
    return jax.shard_map(
        local,
        mesh=split_mesh,
        in_specs=(
            P(CTX, CH),
            P(CTX, CH),
            P(CTX, CH),
            P(None, None, CH),
            P(CH, None),
            P(CH),
            P(CTX, CH),
            P(CTX),
            P(CTX, CH),
        ),
        out_specs=(P(CTX, CH), P(CTX, CH), P(CTX, CH), P(CTX, CH)),
        check_vma=False,
    )
```

```python
import jax
import jax.numpy as jnp
from jax import lax
from jax.sharding import Mesh, PartitionSpec as P

HOPS = 3
CHIPS = ("zl", "y")
CTX = ("zl", "y", "core")
CH = ("zh", "x")


def gather_weight(out_weight, chip_count):
    spread = jnp.broadcast_to(out_weight[None], (chip_count,) + out_weight.shape)
    mine = lax.all_to_all(spread, CHIPS, 0, 0, tiled=True).reshape(-1, out_weight.shape[1])
    other = lax.ppermute(mine, "core", [(0, 1), (1, 0)])
    return mine, other, lax.axis_index("core")


def shifted(array, axis, by):
    size = lax.axis_size(axis)
    pairs = [(i, i + by) for i in range(size) if 0 <= i + by < size]
    return lax.ppermute(array, axis, pairs)


def toeplitz_tiles(long_filter, row_count, hop_count):
    group_count, span_len = long_filter.shape
    padded = jnp.concatenate(
        [
            jnp.zeros((group_count, row_count), long_filter.dtype),
            long_filter,
            jnp.zeros((group_count, (hop_count + 3) * row_count - span_len), long_filter.dtype),
        ],
        axis=1,
    )
    tiles_list = []
    for distance in range(hop_count + 1):
        window = padded[:, distance * row_count + 1 : distance * row_count + 1 + 2 * row_count]
        cyclic = jnp.concatenate(
            [
                window[:, row_count - 1 : 2 * row_count - 1],
                jnp.zeros((group_count, 1), window.dtype),
                window[:, : row_count - 1],
            ],
            axis=1,
        )
        repeated = jnp.tile(cyclic, (1, row_count))[:, : row_count * (2 * row_count - 1)]
        tiles_list.append(
            repeated.reshape(group_count, row_count, 2 * row_count - 1)[:, :, :row_count]
        )
    return tiles_list


def apply_forward(band_tile, source):
    row_count, channels = source.shape
    grouped = source.reshape(row_count, band_tile.shape[0], -1)
    return jnp.einsum(
        "gst,sgc->tgc", band_tile, grouped, preferred_element_type=jnp.float32
    ).reshape(row_count, channels)


def apply_adjoint(band_tile, source):
    row_count, channels = source.shape
    grouped = source.reshape(row_count, band_tile.shape[0], -1)
    return jnp.einsum(
        "gst,tgc->sgc", band_tile, grouped, preferred_element_type=jnp.float32
    ).reshape(row_count, channels)


def causal_taps(extended, weights, ext_ids, doc_ids):
    row_count = doc_ids.shape[0]
    summed = jnp.zeros((row_count, extended.shape[1]), jnp.float32)
    for offset in range(3):
        first_row = 2 - offset
        same_doc = ext_ids[first_row : first_row + row_count] == doc_ids
        summed = summed + jnp.where(
            same_doc[:, None],
            weights[offset][None, :]
            * extended[first_row : first_row + row_count].astype(jnp.float32),
            0.0,
        )
    return summed


def anti_taps(extended, weights, ext_ids, doc_ids):
    row_count = doc_ids.shape[0]
    summed = jnp.zeros((row_count, extended.shape[1]), jnp.float32)
    for offset in range(3):
        same_doc = ext_ids[offset : offset + row_count] == doc_ids
        summed = summed + jnp.where(
            same_doc[:, None],
            weights[offset][None, :] * extended[offset : offset + row_count].astype(jnp.float32),
            0.0,
        )
    return summed


def local(
    query_in,
    key_in,
    value_in,
    short_weight,
    long_filter,
    skip_weight,
    out_weight,
    doc_ids,
    out_grad,
):
    row_count, channels = query_in.shape
    before_ids = shifted(doc_ids[-2:] + 1, CTX, 1) - 1
    after_ids = shifted(doc_ids[:2] + 1, CTX, -1) - 1
    first_id = doc_ids[0]
    last_id = doc_ids[-1]
    prev_last = before_ids[1]
    next_first = after_ids[0]
    single_doc = first_id == last_id
    joins_next = next_first == last_id
    joins_prev = prev_last == first_id
    prev_rows = shifted((query_in[-2:], key_in[-2:], value_in[-2:]), CTX, 1)
    back_ids = jnp.concatenate([before_ids, doc_ids])
    query_short = causal_taps(
        jnp.concatenate([prev_rows[0], query_in]), short_weight[0], back_ids, doc_ids
    )
    key_short = causal_taps(
        jnp.concatenate([prev_rows[1], key_in]), short_weight[1], back_ids, doc_ids
    )
    value_short = causal_taps(
        jnp.concatenate([prev_rows[2], value_in]), short_weight[2], back_ids, doc_ids
    )
    gated = (key_short * value_short).astype(jnp.bfloat16)
    tiles_list = toeplitz_tiles(long_filter, row_count, HOPS)
    same_doc = doc_ids[:, None] == doc_ids[None, :]
    diagonal = jnp.where(same_doc[None], tiles_list[0], jnp.zeros((), tiles_list[0].dtype))
    head_rows = (doc_ids == first_id)[:, None]
    tail_rows = (doc_ids == last_id)[:, None]
    zero_half = jnp.zeros((), gated.dtype)

    def cross_term(is_live, product, band_tile, source):
        summand = jnp.where(is_live, product(band_tile, source), 0.0)
        return summand

    mixed = apply_forward(diagonal, gated) + skip_weight[None, :] * gated.astype(jnp.float32)
    own_tail = jnp.where(tail_rows, gated, zero_half)
    moving = jnp.where(joins_next, own_tail, zero_half)
    for distance in range(1, HOPS + 1):
        moving = shifted(moving, CTX, 1)
        is_live = jnp.any(moving != 0)
        mixed = mixed + jnp.where(
            head_rows, cross_term(is_live, apply_forward, tiles_list[distance], moving), 0.0
        )
        moving = jnp.where(single_doc & joins_next, moving, zero_half)
    pre_gate = (query_short * mixed).astype(jnp.bfloat16)
    pair_size = lax.axis_size("core")
    chip_count = lax.axis_size(CHIPS)
    weight_rows, weight_rows_other, core_index = gather_weight(out_weight, chip_count)
    ch_count = lax.axis_size(CH)
    on_first = core_index == 0
    dims = (((1,), (1,)), ((), ()))
    block_chips = chip_count // ch_count
    part_mine = lax.dot_general(
        weight_rows, out_grad, dims, preferred_element_type=jnp.float32
    ).reshape(ch_count, 1, block_chips, -1, row_count)
    part_other = lax.dot_general(
        weight_rows_other, out_grad, dims, preferred_element_type=jnp.float32
    ).reshape(ch_count, 1, block_chips, -1, row_count)
    sent = jnp.concatenate([part_mine, part_other], axis=1)
    received = lax.all_to_all(sent, CH, 0, 0, tiled=True)
    pre_gate, mixed, received = lax.optimization_barrier((pre_gate, mixed, received))
    spread = jnp.broadcast_to(pre_gate[None], (ch_count,) + pre_gate.shape)
    gathered = lax.all_to_all(spread, CH, 0, 0, tiled=True).reshape(
        ch_count, row_count, channels
    )
    full_pre = jnp.transpose(gathered, (1, 0, 2)).reshape(
        row_count, chip_count, pair_size, out_weight.shape[0]
    )
    pre_first = full_pre[:, :, 0].reshape(row_count, -1)
    pre_second = full_pre[:, :, 1].reshape(row_count, -1)
    pre_mine = jnp.where(on_first, pre_first, pre_second)
    pre_other = jnp.where(on_first, pre_second, pre_first)
    out_sum = jnp.dot(pre_mine, weight_rows, preferred_element_type=jnp.float32) + jnp.dot(
        pre_other, weight_rows_other, preferred_element_type=jnp.float32
    )
    summed = jnp.sum(received, axis=0)
    cols_mine, cols_other = summed[0][:, None], summed[1][:, None]
    grad_cols = jnp.where(
        on_first,
        jnp.concatenate([cols_mine, cols_other], axis=1),
        jnp.concatenate([cols_other, cols_mine], axis=1),
    ).reshape(-1, row_count)
    layer_out = out_sum.astype(jnp.bfloat16)
    grad_pre = jnp.transpose(grad_cols)
    grad_query_short = (grad_pre * mixed).astype(jnp.bfloat16)
    grad_mixed = (grad_pre * query_short).astype(jnp.bfloat16)
    own_head = jnp.where(head_rows, grad_mixed, zero_half)
    grad_gated = apply_adjoint(diagonal, grad_mixed) + skip_weight[None, :] * grad_mixed.astype(
        jnp.float32
    )
    moving_back = jnp.where(joins_prev, own_head, zero_half)
    for distance in range(1, HOPS + 1):
        moving_back = shifted(moving_back, CTX, -1)
        is_live = jnp.any(moving_back != 0)
        grad_gated = grad_gated + jnp.where(
            tail_rows, cross_term(is_live, apply_adjoint, tiles_list[distance], moving_back), 0.0
        )
        moving_back = jnp.where(single_doc & joins_prev, moving_back, zero_half)
    grad_key_short = (grad_gated * value_short).astype(jnp.bfloat16)
    grad_value_short = (grad_gated * key_short).astype(jnp.bfloat16)
    next_rows = shifted((grad_query_short[:2], grad_key_short[:2], grad_value_short[:2]), CTX, -1)
    ahead_ids = jnp.concatenate([doc_ids, after_ids])
    grad_query = anti_taps(
        jnp.concatenate([grad_query_short, next_rows[0]]), short_weight[0], ahead_ids, doc_ids
    ).astype(jnp.bfloat16)
    grad_key = anti_taps(
        jnp.concatenate([grad_key_short, next_rows[1]]), short_weight[1], ahead_ids, doc_ids
    ).astype(jnp.bfloat16)
    grad_value = anti_taps(
        jnp.concatenate([grad_value_short, next_rows[2]]), short_weight[2], ahead_ids, doc_ids
    ).astype(jnp.bfloat16)
    return (layer_out, grad_query, grad_key, grad_value)


def solution(mesh):
    zl, y, core = 4, 8, 2
    split_mesh = Mesh(
        mesh.devices.reshape(zl, y, core, mesh.devices.shape[1] // 4, 4),
        ("zl", "y", "core", "zh", "x"),
    )
    return jax.shard_map(
        local,
        mesh=split_mesh,
        in_specs=(
            P(CTX, CH),
            P(CTX, CH),
            P(CTX, CH),
            P(None, None, CH),
            P(CH, None),
            P(CH),
            P(CTX, CH),
            P(CTX),
            P(CTX, CH),
        ),
        out_specs=(P(CTX, CH), P(CTX, CH), P(CTX, CH), P(CTX, CH)),
        check_vma=False,
    )
```

```python
import jax
import jax.numpy as jnp
from jax import lax
from jax.sharding import Mesh, PartitionSpec as P

HOPS = 3
CHIPS = ("zl", "y")
CTX = ("zl", "y", "core")
CH = ("zh", "x")


def gather_weight(out_weight, chip_count):
    spread = jnp.broadcast_to(out_weight[None], (chip_count,) + out_weight.shape)
    mine = lax.all_to_all(spread, CHIPS, 0, 0, tiled=True).reshape(-1, out_weight.shape[1])
    other = lax.ppermute(mine, "core", [(0, 1), (1, 0)])
    return mine, other, lax.axis_index("core")


def shifted(array, axis, by):
    size = lax.axis_size(axis)
    pairs = [(i, i + by) for i in range(size) if 0 <= i + by < size]
    return lax.ppermute(array, axis, pairs)


def toeplitz_tiles(long_filter, row_count, hop_count):
    group_count, span_len = long_filter.shape
    padded = jnp.concatenate(
        [
            jnp.zeros((group_count, row_count), long_filter.dtype),
            long_filter,
            jnp.zeros((group_count, (hop_count + 3) * row_count - span_len), long_filter.dtype),
        ],
        axis=1,
    )
    tiles_list = []
    for distance in range(hop_count + 1):
        window = padded[:, distance * row_count + 1 : distance * row_count + 1 + 2 * row_count]
        cyclic = jnp.concatenate(
            [
                window[:, row_count - 1 : 2 * row_count - 1],
                jnp.zeros((group_count, 1), window.dtype),
                window[:, : row_count - 1],
            ],
            axis=1,
        )
        repeated = jnp.tile(cyclic, (1, row_count))[:, : row_count * (2 * row_count - 1)]
        tiles_list.append(
            repeated.reshape(group_count, row_count, 2 * row_count - 1)[:, :, :row_count]
        )
    return tiles_list


def apply_forward(band_tile, source):
    row_count, channels = source.shape
    grouped = source.reshape(row_count, band_tile.shape[0], -1)
    return jnp.einsum(
        "gst,sgc->tgc", band_tile, grouped, preferred_element_type=jnp.float32
    ).reshape(row_count, channels)


def apply_adjoint(band_tile, source):
    row_count, channels = source.shape
    grouped = source.reshape(row_count, band_tile.shape[0], -1)
    return jnp.einsum(
        "gst,tgc->sgc", band_tile, grouped, preferred_element_type=jnp.float32
    ).reshape(row_count, channels)


def tagged(rows, doc_id):
    tag = jnp.full((1, rows.shape[1]), doc_id + 1, rows.dtype)
    return jnp.concatenate([rows, tag])


def untagged(block):
    return block[:-1], block[-1, 0].astype(jnp.int32) - 1


def causal_taps(extended, weights, ext_ids, doc_ids):
    row_count = doc_ids.shape[0]
    summed = jnp.zeros((row_count, extended.shape[1]), jnp.float32)
    for offset in range(3):
        first_row = 2 - offset
        same_doc = ext_ids[first_row : first_row + row_count] == doc_ids
        summed = summed + jnp.where(
            same_doc[:, None],
            weights[offset][None, :]
            * extended[first_row : first_row + row_count].astype(jnp.float32),
            0.0,
        )
    return summed


def anti_taps(extended, weights, ext_ids, doc_ids):
    row_count = doc_ids.shape[0]
    summed = jnp.zeros((row_count, extended.shape[1]), jnp.float32)
    for offset in range(3):
        same_doc = ext_ids[offset : offset + row_count] == doc_ids
        summed = summed + jnp.where(
            same_doc[:, None],
            weights[offset][None, :] * extended[offset : offset + row_count].astype(jnp.float32),
            0.0,
        )
    return summed


def local(
    query_in,
    key_in,
    value_in,
    short_weight,
    long_filter,
    skip_weight,
    out_weight,
    doc_ids,
    out_grad,
):
    row_count, channels = query_in.shape
    before_ids = shifted(doc_ids[-2:] + 1, CTX, 1) - 1
    after_ids = shifted(doc_ids[:2] + 1, CTX, -1) - 1
    first_id = doc_ids[0]
    last_id = doc_ids[-1]
    prev_last = before_ids[1]
    next_first = after_ids[0]
    single_doc = first_id == last_id
    joins_next = next_first == last_id
    joins_prev = prev_last == first_id
    prev_rows = shifted((query_in[-2:], key_in[-2:], value_in[-2:]), CTX, 1)
    back_ids = jnp.concatenate([before_ids, doc_ids])
    query_short = causal_taps(
        jnp.concatenate([prev_rows[0], query_in]), short_weight[0], back_ids, doc_ids
    )
    key_short = causal_taps(
        jnp.concatenate([prev_rows[1], key_in]), short_weight[1], back_ids, doc_ids
    )
    value_short = causal_taps(
        jnp.concatenate([prev_rows[2], value_in]), short_weight[2], back_ids, doc_ids
    )
    gated = (key_short * value_short).astype(jnp.bfloat16)
    tiles_list = toeplitz_tiles(long_filter, row_count, HOPS)
    same_doc = doc_ids[:, None] == doc_ids[None, :]
    diagonal = jnp.where(same_doc[None], tiles_list[0], jnp.zeros((), tiles_list[0].dtype))
    head_rows = (doc_ids == first_id)[:, None]
    tail_rows = (doc_ids == last_id)[:, None]
    zero_half = jnp.zeros((), gated.dtype)

    def cross_term(is_live, product, band_tile, source):
        summand = jnp.where(is_live, product(band_tile, source), 0.0)
        return summand

    mixed = apply_forward(diagonal, gated) + skip_weight[None, :] * gated.astype(jnp.float32)
    own_tail = jnp.where(tail_rows, gated, zero_half)
    moving = jnp.where(joins_next, own_tail, zero_half)
    for distance in range(1, HOPS + 1):
        moving = shifted(moving, CTX, 1)
        is_live = jnp.any(moving != 0)
        mixed = mixed + jnp.where(
            head_rows, cross_term(is_live, apply_forward, tiles_list[distance], moving), 0.0
        )
        moving = jnp.where(single_doc & joins_next, moving, zero_half)
    pre_gate = (query_short * mixed).astype(jnp.bfloat16)
    pair_size = lax.axis_size("core")
    chip_count = lax.axis_size(CHIPS)
    weight_rows, weight_rows_other, core_index = gather_weight(out_weight, chip_count)
    ch_count = lax.axis_size(CH)
    on_first = core_index == 0
    dims = (((1,), (1,)), ((), ()))
    block_chips = chip_count // ch_count
    part_mine = lax.dot_general(
        weight_rows, out_grad, dims, preferred_element_type=jnp.float32
    ).reshape(ch_count, 1, block_chips, -1, row_count)
    part_other = lax.dot_general(
        weight_rows_other, out_grad, dims, preferred_element_type=jnp.float32
    ).reshape(ch_count, 1, block_chips, -1, row_count)
    sent = jnp.concatenate([part_mine, part_other], axis=1)
    received = lax.all_to_all(sent, CH, 0, 0, tiled=True)
    pre_gate, mixed, received = lax.optimization_barrier((pre_gate, mixed, received))
    spread = jnp.broadcast_to(pre_gate[None], (ch_count,) + pre_gate.shape)
    gathered = lax.all_to_all(spread, CH, 0, 0, tiled=True).reshape(
        ch_count, row_count, channels
    )
    full_pre = jnp.transpose(gathered, (1, 0, 2)).reshape(
        row_count, chip_count, pair_size, out_weight.shape[0]
    )
    pre_first = full_pre[:, :, 0].reshape(row_count, -1)
    pre_second = full_pre[:, :, 1].reshape(row_count, -1)
    pre_mine = jnp.where(on_first, pre_first, pre_second)
    pre_other = jnp.where(on_first, pre_second, pre_first)
    out_sum = jnp.dot(pre_mine, weight_rows, preferred_element_type=jnp.float32) + jnp.dot(
        pre_other, weight_rows_other, preferred_element_type=jnp.float32
    )
    summed = jnp.sum(received, axis=0)
    cols_mine, cols_other = summed[0][:, None], summed[1][:, None]
    grad_cols = jnp.where(
        on_first,
        jnp.concatenate([cols_mine, cols_other], axis=1),
        jnp.concatenate([cols_other, cols_mine], axis=1),
    ).reshape(-1, row_count)
    layer_out = out_sum.astype(jnp.bfloat16)
    grad_pre = jnp.transpose(grad_cols)
    grad_query_short = (grad_pre * mixed).astype(jnp.bfloat16)
    grad_mixed = (grad_pre * query_short).astype(jnp.bfloat16)
    own_head = jnp.where(head_rows, grad_mixed, zero_half)
    grad_gated = apply_adjoint(diagonal, grad_mixed) + skip_weight[None, :] * grad_mixed.astype(
        jnp.float32
    )
    own_head = tagged(own_head, first_id)
    for distance in range(1, HOPS + 1):
        moving_back, source_id = untagged(shifted(own_head, CTX, -distance))
        grad_gated = grad_gated + jnp.where(
            tail_rows & (source_id == last_id),
            apply_adjoint(tiles_list[distance], moving_back),
            0.0,
        )
    grad_key_short = (grad_gated * value_short).astype(jnp.bfloat16)
    grad_value_short = (grad_gated * key_short).astype(jnp.bfloat16)
    next_rows = shifted((grad_query_short[:2], grad_key_short[:2], grad_value_short[:2]), CTX, -1)
    ahead_ids = jnp.concatenate([doc_ids, after_ids])
    grad_query = anti_taps(
        jnp.concatenate([grad_query_short, next_rows[0]]), short_weight[0], ahead_ids, doc_ids
    ).astype(jnp.bfloat16)
    grad_key = anti_taps(
        jnp.concatenate([grad_key_short, next_rows[1]]), short_weight[1], ahead_ids, doc_ids
    ).astype(jnp.bfloat16)
    grad_value = anti_taps(
        jnp.concatenate([grad_value_short, next_rows[2]]), short_weight[2], ahead_ids, doc_ids
    ).astype(jnp.bfloat16)
    return (layer_out, grad_query, grad_key, grad_value)


def solution(mesh):
    zl, y, core = 4, 8, 2
    split_mesh = Mesh(
        mesh.devices.reshape(zl, y, core, mesh.devices.shape[1] // 4, 4),
        ("zl", "y", "core", "zh", "x"),
    )
    return jax.shard_map(
        local,
        mesh=split_mesh,
        in_specs=(
            P(CTX, CH),
            P(CTX, CH),
            P(CTX, CH),
            P(None, None, CH),
            P(CH, None),
            P(CH),
            P(CTX, CH),
            P(CTX),
            P(CTX, CH),
        ),
        out_specs=(P(CTX, CH), P(CTX, CH), P(CTX, CH), P(CTX, CH)),
        check_vma=False,
    )
```

```python
import jax
import jax.numpy as jnp
from jax import lax
from jax.sharding import Mesh, PartitionSpec as P

HOPS = 3
CHIPS = ("zl", "y")
CTX = ("zl", "y", "core")
CH = ("zh", "x")


def gather_weight(out_weight, chip_count):
    spread = jnp.broadcast_to(out_weight[None], (chip_count,) + out_weight.shape)
    mine = lax.all_to_all(spread, CHIPS, 0, 0, tiled=True).reshape(-1, out_weight.shape[1])
    other = lax.ppermute(mine, "core", [(0, 1), (1, 0)])
    return mine, other, lax.axis_index("core")


def shifted(array, axis, by):
    size = lax.axis_size(axis)
    pairs = [(i, i + by) for i in range(size) if 0 <= i + by < size]
    return lax.ppermute(array, axis, pairs)


def toeplitz_tiles(long_filter, row_count, hop_count):
    group_count, span_len = long_filter.shape
    padded = jnp.concatenate(
        [
            jnp.zeros((group_count, row_count), long_filter.dtype),
            long_filter,
            jnp.zeros((group_count, (hop_count + 3) * row_count - span_len), long_filter.dtype),
        ],
        axis=1,
    )
    tiles_list = []
    for distance in range(hop_count + 1):
        window = padded[:, distance * row_count + 1 : distance * row_count + 1 + 2 * row_count]
        cyclic = jnp.concatenate(
            [
                window[:, row_count - 1 : 2 * row_count - 1],
                jnp.zeros((group_count, 1), window.dtype),
                window[:, : row_count - 1],
            ],
            axis=1,
        )
        repeated = jnp.tile(cyclic, (1, row_count))[:, : row_count * (2 * row_count - 1)]
        tiles_list.append(
            repeated.reshape(group_count, row_count, 2 * row_count - 1)[:, :, :row_count]
        )
    return tiles_list


def apply_forward(band_tile, source):
    row_count, channels = source.shape
    grouped = source.reshape(row_count, band_tile.shape[0], -1)
    return jnp.einsum(
        "gst,sgc->tgc", band_tile, grouped, preferred_element_type=jnp.float32
    ).reshape(row_count, channels)


def apply_adjoint(band_tile, source):
    row_count, channels = source.shape
    grouped = source.reshape(row_count, band_tile.shape[0], -1)
    return jnp.einsum(
        "gst,tgc->sgc", band_tile, grouped, preferred_element_type=jnp.float32
    ).reshape(row_count, channels)


def causal_taps(extended, weights, ext_ids, doc_ids):
    row_count = doc_ids.shape[0]
    summed = jnp.zeros((row_count, extended.shape[1]), jnp.float32)
    for offset in range(3):
        first_row = 2 - offset
        same_doc = ext_ids[first_row : first_row + row_count] == doc_ids
        summed = summed + jnp.where(
            same_doc[:, None],
            weights[offset][None, :]
            * extended[first_row : first_row + row_count].astype(jnp.float32),
            0.0,
        )
    return summed


def anti_taps(extended, weights, ext_ids, doc_ids):
    row_count = doc_ids.shape[0]
    summed = jnp.zeros((row_count, extended.shape[1]), jnp.float32)
    for offset in range(3):
        same_doc = ext_ids[offset : offset + row_count] == doc_ids
        summed = summed + jnp.where(
            same_doc[:, None],
            weights[offset][None, :] * extended[offset : offset + row_count].astype(jnp.float32),
            0.0,
        )
    return summed


def local(
    query_in,
    key_in,
    value_in,
    short_weight,
    long_filter,
    skip_weight,
    out_weight,
    doc_ids,
    out_grad,
):
    row_count, channels = query_in.shape
    before_ids = shifted(doc_ids[-2:] + 1, CTX, 1) - 1
    after_ids = shifted(doc_ids[:2] + 1, CTX, -1) - 1
    first_id = doc_ids[0]
    last_id = doc_ids[-1]
    prev_last = before_ids[1]
    next_first = after_ids[0]
    single_doc = first_id == last_id
    joins_next = next_first == last_id
    joins_prev = prev_last == first_id
    prev_rows = shifted((query_in[-2:], key_in[-2:], value_in[-2:]), CTX, 1)
    back_ids = jnp.concatenate([before_ids, doc_ids])
    query_short = causal_taps(
        jnp.concatenate([prev_rows[0], query_in]), short_weight[0], back_ids, doc_ids
    )
    key_short = causal_taps(
        jnp.concatenate([prev_rows[1], key_in]), short_weight[1], back_ids, doc_ids
    )
    value_short = causal_taps(
        jnp.concatenate([prev_rows[2], value_in]), short_weight[2], back_ids, doc_ids
    )
    gated = (key_short * value_short).astype(jnp.bfloat16)
    tiles_list = toeplitz_tiles(long_filter, row_count, HOPS)
    same_doc = doc_ids[:, None] == doc_ids[None, :]
    diagonal = jnp.where(same_doc[None], tiles_list[0], jnp.zeros((), tiles_list[0].dtype))
    head_rows = (doc_ids == first_id)[:, None]
    tail_rows = (doc_ids == last_id)[:, None]
    zero_half = jnp.zeros((), gated.dtype)

    def cross_term(is_live, product, band_tile, source):
        summand = jnp.where(is_live, product(band_tile, source), 0.0)
        return summand

    mixed = apply_forward(diagonal, gated) + skip_weight[None, :] * gated.astype(jnp.float32)
    own_tail = jnp.where(tail_rows, gated, zero_half)
    moving = jnp.where(joins_next, own_tail, zero_half)
    for distance in range(1, HOPS + 1):
        moving = shifted(moving, CTX, 1)
        is_live = jnp.any(moving != 0)
        mixed = mixed + jnp.where(
            head_rows, cross_term(is_live, apply_forward, tiles_list[distance], moving), 0.0
        )
        moving = jnp.where(single_doc & joins_next, moving, zero_half)
    pre_gate = (query_short * mixed).astype(jnp.bfloat16)
    pair_size = lax.axis_size("core")
    chip_count = lax.axis_size(CHIPS)
    weight_rows, weight_rows_other, core_index = gather_weight(out_weight, chip_count)
    ch_count = lax.axis_size(CH)
    on_first = core_index == 0
    weight_first = jnp.where(on_first, weight_rows, weight_rows_other)
    weight_second = jnp.where(on_first, weight_rows_other, weight_rows)
    dims = (((1,), (1,)), ((), ()))
    block_chips = chip_count // ch_count
    part_mine = lax.dot_general(
        weight_rows, out_grad, dims, preferred_element_type=jnp.float32
    ).reshape(ch_count, 1, block_chips, -1, row_count)
    part_other = lax.dot_general(
        weight_rows_other, out_grad, dims, preferred_element_type=jnp.float32
    ).reshape(ch_count, 1, block_chips, -1, row_count)
    sent = jnp.concatenate([part_mine, part_other], axis=1)
    received = lax.all_to_all(sent, CH, 0, 0, tiled=True)
    pre_gate, mixed, received = lax.optimization_barrier((pre_gate, mixed, received))
    spread = jnp.broadcast_to(pre_gate[None], (ch_count,) + pre_gate.shape)
    gathered = lax.all_to_all(spread, CH, 0, 0, tiled=True).reshape(
        ch_count, row_count, channels
    )
    full_pre = jnp.transpose(gathered, (1, 0, 2)).reshape(
        row_count, chip_count, pair_size, out_weight.shape[0]
    )
    pre_first = full_pre[:, :, 0].reshape(row_count, -1)
    pre_second = full_pre[:, :, 1].reshape(row_count, -1)
    out_sum = jnp.dot(pre_first, weight_first, preferred_element_type=jnp.float32) + jnp.dot(
        pre_second, weight_second, preferred_element_type=jnp.float32
    )
    summed = jnp.sum(received, axis=0)
    cols_mine, cols_other = summed[0][:, None], summed[1][:, None]
    grad_cols = jnp.where(
        on_first,
        jnp.concatenate([cols_mine, cols_other], axis=1),
        jnp.concatenate([cols_other, cols_mine], axis=1),
    ).reshape(-1, row_count)
    layer_out = out_sum.astype(jnp.bfloat16)
    grad_pre = jnp.transpose(grad_cols)
    grad_query_short = (grad_pre * mixed).astype(jnp.bfloat16)
    grad_mixed = (grad_pre * query_short).astype(jnp.bfloat16)
    own_head = jnp.where(head_rows, grad_mixed, zero_half)
    grad_gated = apply_adjoint(diagonal, grad_mixed) + skip_weight[None, :] * grad_mixed.astype(
        jnp.float32
    )
    moving_back = jnp.where(joins_prev, own_head, zero_half)
    for distance in range(1, HOPS + 1):
        moving_back = shifted(moving_back, CTX, -1)
        is_live = jnp.any(moving_back != 0)
        grad_gated = grad_gated + jnp.where(
            tail_rows, cross_term(is_live, apply_adjoint, tiles_list[distance], moving_back), 0.0
        )
        moving_back = jnp.where(single_doc & joins_prev, moving_back, zero_half)
    grad_key_short = (grad_gated * value_short).astype(jnp.bfloat16)
    grad_value_short = (grad_gated * key_short).astype(jnp.bfloat16)
    next_rows = shifted((grad_query_short[:2], grad_key_short[:2], grad_value_short[:2]), CTX, -1)
    ahead_ids = jnp.concatenate([doc_ids, after_ids])
    grad_query = anti_taps(
        jnp.concatenate([grad_query_short, next_rows[0]]), short_weight[0], ahead_ids, doc_ids
    ).astype(jnp.bfloat16)
    grad_key = anti_taps(
        jnp.concatenate([grad_key_short, next_rows[1]]), short_weight[1], ahead_ids, doc_ids
    ).astype(jnp.bfloat16)
    grad_value = anti_taps(
        jnp.concatenate([grad_value_short, next_rows[2]]), short_weight[2], ahead_ids, doc_ids
    ).astype(jnp.bfloat16)
    return (layer_out, grad_query, grad_key, grad_value)


def solution(mesh):
    zl, y, core = 4, 8, 2
    split_mesh = Mesh(
        mesh.devices.reshape(zl, y, core, mesh.devices.shape[1] // 4, 4),
        ("zl", "y", "core", "zh", "x"),
    )
    return jax.shard_map(
        local,
        mesh=split_mesh,
        in_specs=(
            P(CTX, CH),
            P(CTX, CH),
            P(CTX, CH),
            P(None, None, CH),
            P(CH, None),
            P(CH),
            P(CTX, CH),
            P(CTX),
            P(CTX, CH),
        ),
        out_specs=(P(CTX, CH), P(CTX, CH), P(CTX, CH), P(CTX, CH)),
        check_vma=False,
    )
```
